32 devices in a mesh: blk: 4 (over x, core), st: 8 (over z, y).
Axes of the slice: x: 2, y: 2, z: 4, core: 2. Of those that a mesh axis runs over, the one named last changes fastest.
Arguments:
- voltages: bfloat16 [2, 4, 512, 34176], P(None, 'blk', 'st'), may hold values from -6 to 6
- filter_coeffs: float32 [12, 128], replicated, may hold values from -1.75 to 1.75
- station_gain: float32 [512], P('st'), may hold values from 0.5 to 5
- flags: int32 [4, 512], P('blk', 'st'), may hold values 0 or 1
- steer_index: int32 [512, 128], replicated, may hold values from 0 to 4095
Outputs:
- beams: bfloat16 [2, 128, 4, 256, 128], P(None, 'st', 'blk')
The draws below stay inside these ranges and needn't reach their ends.
All inputs are finite; a program needn't handle non-finite values. No bound on the sum of `flags` on one device may be relied on, other than what follows from the above.
Results may differ from the reference program's by a relative error of at most 0.0074.
Values may be sent and summed in bfloat16 or wider, within the bound.
No kernel may reach another device: no remote copies, remote signals or barrier semaphores. Data moves between devices by JAX's collectives and lax.ppermute only.
A program may use at most 320 MiB of HBM per device.

```python
import math
import jax
import jax.numpy as jnp
from jax import lax

S = 512
C = 128
NB = 128
TAPS = 12
PHASES = 4096
SPEC = 256
BLOCKS = 4
WIN = 34176


def with_ends(result, stream_key, least, high):
    extent = result.shape
    place = [jax.random.randint(jax.random.fold_in(stream_key, axis), (), 0, extent[axis]) for axis in range(len(extent))]
    result = result.at[tuple(place)].set(least)
    longest = extent.index(max(extent))
    place[longest] = (place[longest] + 1) % extent[longest]
    return result.at[tuple(place)].set(high)


def levels(own_key, shape, cuts, smallest, largest):
    level, own = 1.0, jax.random.fold_in(own_key, 6)
    for dim, parts in cuts:
        heights = jnp.exp(jax.random.uniform(jax.random.fold_in(own, dim), (parts,), jnp.float32, smallest / len(cuts), largest / len(cuts)))
        level = level * jnp.repeat(heights, shape[dim] // parts).reshape([-1 if axis == dim else 1 for axis in range(len(shape))])
    return level


def scatter_about(rng, extent, deviation, most, cuts=(), held_as=jnp.bfloat16):
    loudness = levels(rng, extent, cuts, -0.22, 0.18) if cuts else 1.0
    result = jax.random.normal(rng, extent, jnp.float32) * deviation * loudness
    return jnp.minimum(jnp.maximum(result, -most), most).astype(held_as)


def setup_inputs(seed: int = 0) -> dict:
    arg_keys = jax.random.split(jax.random.key(seed), 6)
    return {
        "voltages": scatter_about(arg_keys[0], (2, BLOCKS, S, WIN), 1.0, 6.0, ((1, 4), (2, 8))),
        "filter_coeffs": scatter_about(arg_keys[1], (TAPS, C), TAPS ** -0.5, 1.75, (), jnp.float32),
        "station_gain": jnp.clip(jnp.exp(math.log(5.0) - 2.3025851 * jax.random.uniform(arg_keys[2], (S,), jnp.float32) ** levels(arg_keys[2], (S,), ((0, 8),), -0.2, 0.2)), 0.5, 5.0),
        "flags": with_ends((jax.random.randint(arg_keys[3], (BLOCKS, S), 0, 8) < 7).astype(jnp.int32), jax.random.fold_in(arg_keys[3], 1), 0, 1),
        "steer_index": with_ends(jax.random.randint(arg_keys[4], (S, NB), 0, PHASES), jax.random.fold_in(arg_keys[4], 1), 0, PHASES - 1).astype(jnp.int32),
    }


def dft_tables(width):
    counter = jnp.arange(width, dtype=jnp.int32)
    product = counter[:, None] * counter[None, :] % width
    angle = product.astype(jnp.float32) * (2.0 * math.pi / width)
    factor = 1.0 / math.sqrt(width)
    return ((jnp.cos(angle) * factor).astype(jnp.bfloat16), (jnp.sin(angle) * factor).astype(jnp.bfloat16))

def polyphase(samples, filter_coeffs, row_gain):
    ntaps = filter_coeffs.shape[0]
    width = filter_coeffs.shape[1]
    grid = samples.astype(jnp.float32).reshape(2, samples.shape[1], -1, width)
    count = grid.shape[2] - ntaps + 1
    filtered = filter_coeffs[0][None, None, None, :] * grid[:, :, 0:count, :]
    for tap_no in range(1, ntaps):
        filtered = filtered + filter_coeffs[tap_no][None, None, None, :] * grid[:, :, tap_no:tap_no + count, :]
    return (filtered * row_gain[None, :, None, None]).astype(jnp.bfloat16)

def transform(filtered, cos_table, sin_table):
    width = cos_table.shape[0]
    flat_re = filtered[0].reshape(-1, width)
    flat_im = filtered[1].reshape(-1, width)
    out_re = jnp.dot(flat_re, cos_table, preferred_element_type=jnp.float32) + jnp.dot(flat_im, sin_table, preferred_element_type=jnp.float32)
    out_im = jnp.dot(flat_im, cos_table, preferred_element_type=jnp.float32) - jnp.dot(flat_re, sin_table, preferred_element_type=jnp.float32)
    return jnp.stack([out_re, out_im]).astype(jnp.bfloat16).reshape(filtered.shape)

def highest(left, right):
    return jnp.dot(left, right, precision=lax.Precision.HIGHEST)

def reference(voltages, filter_coeffs, station_gain, flags, steer_index):
    cos_table, sin_table = dft_tables(C)
    pieces = []
    for block_no in range(BLOCKS):
        row_gain = station_gain * flags[block_no].astype(jnp.float32)
        filtered = polyphase(voltages[:, block_no], filter_coeffs, row_gain)
        pieces.append(transform(filtered, cos_table, sin_table))
    spectra = jnp.stack(pieces, 2).reshape(2, S, BLOCKS * SPEC, C)
    channel_major = jnp.transpose(spectra, (3, 0, 1, 2))

    def one_channel(item):
        spec_k, channel_no = item
        spec_re = spec_k[0]
        spec_im = spec_k[1]
        cov_re = jnp.dot(spec_re, spec_re.T, preferred_element_type=jnp.float32) + jnp.dot(spec_im, spec_im.T, preferred_element_type=jnp.float32)
        cov_im = jnp.dot(spec_im, spec_re.T, preferred_element_type=jnp.float32) - jnp.dot(spec_re, spec_im.T, preferred_element_type=jnp.float32)
        cov_re = cov_re / (BLOCKS * SPEC)
        cov_im = cov_im / (BLOCKS * SPEC)
        load = jnp.sum(jnp.diagonal(cov_re)) / S + 1e-05
        diag_total = (jnp.diagonal(cov_re) + load)[:, None]
        phase_int = steer_index * (channel_no + 1) % PHASES
        angle = phase_int.astype(jnp.float32) * (2.0 * math.pi / PHASES)
        steer_re = jnp.cos(angle)
        steer_im = jnp.sin(angle)
        weight_re = steer_re / diag_total
        weight_im = steer_im / diag_total
        for sweep_no in range(2):
            prod_re = highest(cov_re, weight_re) - highest(cov_im, weight_im)
            prod_im = highest(cov_re, weight_im) + highest(cov_im, weight_re)
            next_re = weight_re + 0.5 * (steer_re - prod_re - load * weight_re) / diag_total
            next_im = weight_im + 0.5 * (steer_im - prod_im - load * weight_im) / diag_total
            weight_re, weight_im = (next_re, next_im)
        half_re = weight_re.astype(jnp.bfloat16)
        half_im = weight_im.astype(jnp.bfloat16)
        beam_re = jnp.dot(half_re.T, spec_re, preferred_element_type=jnp.float32) + jnp.dot(half_im.T, spec_im, preferred_element_type=jnp.float32)
        beam_im = jnp.dot(half_re.T, spec_im, preferred_element_type=jnp.float32) - jnp.dot(half_im.T, spec_re, preferred_element_type=jnp.float32)
        factor = 1.0 / math.sqrt(S)
        return (jnp.stack([beam_re, beam_im]) * factor).astype(jnp.bfloat16)
    results = lax.map(one_channel, (channel_major, jnp.arange(C, dtype=jnp.int32)))
    results = results.reshape(C, 2, NB, BLOCKS, SPEC)
    return jnp.transpose(results, (1, 2, 3, 4, 0))
```

```python
import math

import jax
import jax.numpy as jnp
from jax import lax
from jax.sharding import PartitionSpec as P

PHASES = 4096
AXES = ("blk", "st")


def dft_tables(width):
    counter = jnp.arange(width, dtype=jnp.int32)
    product = counter[:, None] * counter[None, :] % width
    angle = product.astype(jnp.float32) * (2.0 * math.pi / width)
    factor = 1.0 / math.sqrt(width)
    return (
        (jnp.cos(angle) * factor).astype(jnp.bfloat16),
        (jnp.sin(angle) * factor).astype(jnp.bfloat16),
    )


def polyphase(samples, filter_coeffs, row_gain):
    ntaps = filter_coeffs.shape[0]
    width = filter_coeffs.shape[1]
    grid = samples.astype(jnp.float32).reshape(2, samples.shape[1], -1, width)
    count = grid.shape[2] - ntaps + 1
    filtered = filter_coeffs[0][None, None, None, :] * grid[:, :, 0:count, :]
    for tap_no in range(1, ntaps):
        filtered = (
            filtered
            + filter_coeffs[tap_no][None, None, None, :] * grid[:, :, tap_no : tap_no + count, :]
        )
    return (filtered * row_gain[None, :, None, None]).astype(jnp.bfloat16)


def transform(filtered, cos_table, sin_table):
    flat_re = filtered[0]
    flat_im = filtered[1]
    dot = lambda a, b: jnp.einsum("stc,ck->stk", a, b, preferred_element_type=jnp.float32)
    out_re = dot(flat_re, cos_table) + dot(flat_im, sin_table)
    out_im = dot(flat_im, cos_table) - dot(flat_re, sin_table)
    return jnp.stack([out_re, out_im]).astype(jnp.bfloat16)


def batched(matrix, vectors):
    return jnp.einsum("ksu,kub->ksb", matrix, vectors, precision=lax.Precision.HIGHEST)


def iterate(rows_re, rows_im, steer_re, steer_im, diag_total, load):
    weight_re = steer_re / diag_total
    weight_im = steer_im / diag_total
    for sweep_no in range(2):
        prod_re = batched(rows_re, weight_re) - batched(rows_im, weight_im)
        prod_im = batched(rows_re, weight_im) + batched(rows_im, weight_re)
        next_re = weight_re + 0.5 * (steer_re - prod_re - load * weight_re) / diag_total
        next_im = weight_im + 0.5 * (steer_im - prod_im - load * weight_im) / diag_total
        weight_re, weight_im = (next_re, next_im)
    return weight_re, weight_im


def local(voltages, filter_coeffs, station_gain, flags, steer_index):
    nblk = lax.axis_size("blk")
    nst = lax.axis_size("st")
    ndev = nblk * nst
    cos_table, sin_table = dft_tables(filter_coeffs.shape[1])
    row_gain = station_gain * flags[0].astype(jnp.float32)
    filtered = polyphase(voltages[:, 0], filter_coeffs, row_gain)
    local_spec = transform(filtered, cos_table, sin_table)
    _, ls, nt, nk = local_spec.shape
    kc = nk // ndev
    send = local_spec.reshape(2, ls, nt, ndev, kc).transpose(3, 4, 0, 1, 2)
    recv = lax.all_to_all(send, AXES, split_axis=0, concat_axis=0, tiled=True)
    recv = recv.reshape(nblk, nst, kc, 2, ls, nt)
    spec = recv.transpose(2, 3, 1, 4, 0, 5).reshape(kc, 2, nst * ls, nblk * nt)
    stations = nst * ls
    counted = nblk * nt
    spec_re = spec[:, 0]
    spec_im = spec[:, 1]
    cdot = lambda a, b: jnp.einsum("kst,kut->ksu", a, b, preferred_element_type=jnp.float32)
    cov_re = cdot(spec_re, spec_re) + cdot(spec_im, spec_im)
    cov_im = cdot(spec_im, spec_re) - cdot(spec_re, spec_im)
    me = lax.axis_index("blk") * nst + lax.axis_index("st")
    channel_ids = me * kc + jnp.arange(kc, dtype=jnp.int32)
    rows_re = cov_re / counted
    rows_im = cov_im / counted
    diag_part = jnp.diagonal(rows_re, axis1=1, axis2=2)
    load = jnp.sum(diag_part, axis=1) / stations + 1e-05
    phase_int = steer_index[None, :, :] * (channel_ids + 1)[:, None, None] % PHASES
    angle = phase_int.astype(jnp.float32) * (2.0 * math.pi / PHASES)
    steer_re = jnp.cos(angle)
    steer_im = jnp.sin(angle)
    load_full = load[:, None, None]
    diag_total = (diag_part + load[:, None])[:, :, None]
    weight_re, weight_im = iterate(rows_re, rows_im, steer_re, steer_im, diag_total, load_full)
    half_re = weight_re.astype(jnp.bfloat16)
    half_im = weight_im.astype(jnp.bfloat16)
    bdot = lambda a, b: jnp.einsum("ksb,kst->kbt", a, b, preferred_element_type=jnp.float32)
    beam_re = bdot(half_re, spec_re) + bdot(half_im, spec_im)
    beam_im = bdot(half_re, spec_im) - bdot(half_im, spec_re)
    factor = 1.0 / math.sqrt(stations)
    beam = (jnp.stack([beam_re, beam_im]) * factor).astype(jnp.bfloat16)
    nb = beam.shape[2]
    bc = nb // nst
    out = beam.reshape(2, kc, nst, bc, nblk, nt).transpose(4, 2, 0, 3, 5, 1)
    out = out.reshape(ndev, 2, bc, nt, kc)
    got = lax.all_to_all(out, AXES, split_axis=0, concat_axis=0, tiled=True)
    got = got.transpose(1, 2, 3, 0, 4).reshape(2, bc, nt, ndev * kc)
    return got[:, :, None]


def fb_transform(filtered, cos_table, sin_table):
    width = cos_table.shape[0]
    flat_re = filtered[0].reshape(-1, width)
    flat_im = filtered[1].reshape(-1, width)
    out_re = jnp.dot(flat_re, cos_table, preferred_element_type=jnp.float32) + jnp.dot(
        flat_im, sin_table, preferred_element_type=jnp.float32
    )
    out_im = jnp.dot(flat_im, cos_table, preferred_element_type=jnp.float32) - jnp.dot(
        flat_re, sin_table, preferred_element_type=jnp.float32
    )
    return jnp.stack([out_re, out_im]).astype(jnp.bfloat16).reshape(filtered.shape)


def fb_batched(matrix, vectors):
    return jnp.einsum("ksu,kub->ksb", matrix, vectors, precision=lax.Precision.HIGHEST)


def fb_iterate(rows_re, rows_im, steer_re, steer_im, diag_total, load, collect, combine):
    weight_re = steer_re / diag_total
    weight_im = steer_im / diag_total
    for sweep_no in range(2):
        full_re, full_im = collect(weight_re, weight_im)
        prod_re = fb_batched(rows_re, full_re) - fb_batched(rows_im, full_im)
        prod_im = fb_batched(rows_re, full_im) + fb_batched(rows_im, full_re)
        prod_re, prod_im = combine(prod_re, prod_im)
        next_re = weight_re + 0.5 * (steer_re - prod_re - load * weight_re) / diag_total
        next_im = weight_im + 0.5 * (steer_im - prod_im - load * weight_im) / diag_total
        weight_re, weight_im = (next_re, next_im)
    return collect(weight_re, weight_im)


def unchanged(part_re, part_im):
    return (part_re, part_im)


def fb_local(voltages, filter_coeffs, station_gain, flags, steer_index):
    cos_table, sin_table = dft_tables(filter_coeffs.shape[1])
    row_gain = station_gain * flags[0].astype(jnp.float32)
    filtered = polyphase(voltages[:, 0], filter_coeffs, row_gain)
    local_spec = fb_transform(filtered, cos_table, sin_table)
    spectra = lax.all_to_all(local_spec, "st", split_axis=3, concat_axis=1, tiled=True)
    stations = spectra.shape[1]
    chans = spectra.shape[3]
    counted = lax.axis_size("blk") * spectra.shape[2]
    spec_re = spectra[0]
    spec_im = spectra[1]
    cov_re = jnp.einsum(
        "stk,utk->ksu", spec_re, spec_re, preferred_element_type=jnp.float32
    ) + jnp.einsum("stk,utk->ksu", spec_im, spec_im, preferred_element_type=jnp.float32)
    cov_im = jnp.einsum(
        "stk,utk->ksu", spec_im, spec_re, preferred_element_type=jnp.float32
    ) - jnp.einsum("stk,utk->ksu", spec_re, spec_im, preferred_element_type=jnp.float32)
    channel_ids = lax.axis_index("st") * chans + jnp.arange(chans, dtype=jnp.int32)
    total_re, total_im = lax.psum((cov_re, cov_im), "blk")
    rows_re = total_re / counted
    rows_im = total_im / counted
    diag_part = jnp.diagonal(rows_re, axis1=1, axis2=2)
    load = jnp.sum(diag_part, axis=1) / stations + 1e-05
    phase_int = steer_index[None, :, :] * (channel_ids + 1)[:, None, None] % PHASES
    angle = phase_int.astype(jnp.float32) * (2.0 * math.pi / PHASES)
    steer_re = jnp.cos(angle)
    steer_im = jnp.sin(angle)
    load_full = load[:, None, None]
    diag_total = (diag_part + load[:, None])[:, :, None]
    weight_re, weight_im = fb_iterate(
        rows_re, rows_im, steer_re, steer_im, diag_total, load_full, unchanged, unchanged
    )
    half_re = weight_re.astype(jnp.bfloat16)
    half_im = weight_im.astype(jnp.bfloat16)
    beam_re = jnp.einsum(
        "ksb,stk->btk", half_re, spec_re, preferred_element_type=jnp.float32
    ) + jnp.einsum("ksb,stk->btk", half_im, spec_im, preferred_element_type=jnp.float32)
    beam_im = jnp.einsum(
        "ksb,stk->btk", half_re, spec_im, preferred_element_type=jnp.float32
    ) - jnp.einsum("ksb,stk->btk", half_im, spec_re, preferred_element_type=jnp.float32)
    factor = 1.0 / math.sqrt(stations)
    beam_local = (jnp.stack([beam_re, beam_im]) * factor).astype(jnp.bfloat16)
    owned = lax.all_to_all(beam_local, "st", split_axis=1, concat_axis=3, tiled=True)
    return owned[:, :, None]


def body(voltages, filter_coeffs, station_gain, flags, steer_index):
    ndev = lax.axis_size("blk") * lax.axis_size("st")
    plan = local if filter_coeffs.shape[1] % ndev == 0 else fb_local
    return plan(voltages, filter_coeffs, station_gain, flags, steer_index)


def solution(mesh):
    return jax.shard_map(
        body,
        mesh=mesh,
        in_specs=(P(None, "blk", "st", None), P(), P("st"), P("blk", "st"), P()),
        out_specs=P(None, "st", "blk", None, None),
        check_vma=False,
    )
```

```python
import math

import jax
import jax.numpy as jnp
from jax import lax
from jax.sharding import PartitionSpec as P

PHASES = 4096
AXES = ("blk", "st")


def dft_tables(width):
    counter = jnp.arange(width, dtype=jnp.int32)
    product = counter[:, None] * counter[None, :] % width
    angle = product.astype(jnp.float32) * (2.0 * math.pi / width)
    factor = 1.0 / math.sqrt(width)
    return (
        (jnp.cos(angle) * factor).astype(jnp.bfloat16),
        (jnp.sin(angle) * factor).astype(jnp.bfloat16),
    )


def polyphase(samples, filter_coeffs, row_gain):
    ntaps = filter_coeffs.shape[0]
    width = filter_coeffs.shape[1]
    grid = samples.astype(jnp.float32).reshape(2, samples.shape[1], -1, width)
    count = grid.shape[2] - ntaps + 1
    filtered = filter_coeffs[0][None, None, None, :] * grid[:, :, 0:count, :]
    for tap_no in range(1, ntaps):
        filtered = (
            filtered
            + filter_coeffs[tap_no][None, None, None, :] * grid[:, :, tap_no : tap_no + count, :]
        )
    return (filtered * row_gain[None, :, None, None]).astype(jnp.bfloat16)


def transform(filtered, cos_table, sin_table):
    flat_re = filtered[0]
    flat_im = filtered[1]
    dot = lambda a, b: jnp.einsum("stc,ck->stk", a, b, preferred_element_type=jnp.float32)
    out_re = dot(flat_re, cos_table) + dot(flat_im, sin_table)
    out_im = dot(flat_im, cos_table) - dot(flat_re, sin_table)
    return jnp.stack([out_re, out_im]).astype(jnp.bfloat16)


def batched(matrix, vectors):
    return jnp.einsum("ksu,kub->ksb", matrix, vectors, precision=lax.Precision.HIGHEST)


def iterate(rows_re, rows_im, steer_re, steer_im, diag_total, load):
    weight_re = steer_re / diag_total
    weight_im = steer_im / diag_total
    for sweep_no in range(2):
        prod_re = batched(rows_re, weight_re) - batched(rows_im, weight_im)
        prod_im = batched(rows_re, weight_im) + batched(rows_im, weight_re)
        next_re = weight_re + 0.5 * (steer_re - prod_re - load * weight_re) / diag_total
        next_im = weight_im + 0.5 * (steer_im - prod_im - load * weight_im) / diag_total
        weight_re, weight_im = (next_re, next_im)
    return weight_re, weight_im


def chunk_count(nt):
    for n in (4, 2):
        if nt % n == 0:
            return n
    return 1


def local(voltages, filter_coeffs, station_gain, flags, steer_index):
    nblk = lax.axis_size("blk")
    nst = lax.axis_size("st")
    ndev = nblk * nst
    ntaps, width = filter_coeffs.shape
    cos_table, sin_table = dft_tables(width)
    row_gain = station_gain * flags[0].astype(jnp.float32)
    samples = voltages[:, 0]
    ls = samples.shape[1]
    nt = samples.shape[2] // width - ntaps + 1
    nk = width
    kc = nk // ndev
    nch = chunk_count(nt)
    tc = nt // nch
    stations = nst * ls
    counted = nblk * nt
    cdot = lambda a, b: jnp.einsum("kst,kut->ksu", a, b, preferred_element_type=jnp.float32)
    specs = []
    cov_re = None
    cov_im = None
    for ch in range(nch):
        t0 = ch * tc
        piece = samples[:, :, t0 * width : (t0 + tc + ntaps - 1) * width]
        filtered = polyphase(piece, filter_coeffs, row_gain)
        local_spec = transform(filtered, cos_table, sin_table)
        send = local_spec.reshape(2, ls, tc, ndev, kc).transpose(3, 4, 0, 1, 2)
        recv = lax.all_to_all(send, AXES, split_axis=0, concat_axis=0, tiled=True)
        recv = recv.reshape(nblk, nst, kc, 2, ls, tc)
        spec = recv.transpose(2, 3, 1, 4, 0, 5).reshape(kc, 2, stations, nblk * tc)
        specs.append(spec)
        spec_re = spec[:, 0]
        spec_im = spec[:, 1]
        part_re = cdot(spec_re, spec_re) + cdot(spec_im, spec_im)
        part_im = cdot(spec_im, spec_re) - cdot(spec_re, spec_im)
        cov_re = part_re if cov_re is None else cov_re + part_re
        cov_im = part_im if cov_im is None else cov_im + part_im
    me = lax.axis_index("blk") * nst + lax.axis_index("st")
    channel_ids = me * kc + jnp.arange(kc, dtype=jnp.int32)
    rows_re = cov_re / counted
    rows_im = cov_im / counted
    eye = jnp.eye(stations, dtype=jnp.float32)
    diag_part = jnp.sum(rows_re * eye[None], axis=2)
    load = jnp.sum(diag_part, axis=1) / stations + 1e-05
    phase_int = steer_index[None, :, :] * (channel_ids + 1)[:, None, None] % PHASES
    angle = phase_int.astype(jnp.float32) * (2.0 * math.pi / PHASES)
    steer_re = jnp.cos(angle)
    steer_im = jnp.sin(angle)
    load_full = load[:, None, None]
    diag_total = (diag_part + load[:, None])[:, :, None]
    weight_re, weight_im = iterate(rows_re, rows_im, steer_re, steer_im, diag_total, load_full)
    half_re = weight_re.astype(jnp.bfloat16)
    half_im = weight_im.astype(jnp.bfloat16)
    bdot = lambda a, b: jnp.einsum("ksb,kst->kbt", a, b, preferred_element_type=jnp.float32)
    factor = 1.0 / math.sqrt(stations)
    nb = half_re.shape[2]
    bc = nb // nst
    outs = []
    for spec in specs:
        spec_re = spec[:, 0]
        spec_im = spec[:, 1]
        beam_re = bdot(half_re, spec_re) + bdot(half_im, spec_im)
        beam_im = bdot(half_re, spec_im) - bdot(half_im, spec_re)
        beam = (jnp.stack([beam_re, beam_im]) * factor).astype(jnp.bfloat16)
        outs.append(beam.reshape(2, kc, nst, bc, nblk, tc))
    beam = jnp.stack(outs, axis=5)
    out = beam.transpose(4, 2, 0, 3, 5, 6, 1).reshape(ndev, 2, bc, nt, kc)
    got = lax.all_to_all(out, AXES, split_axis=0, concat_axis=0, tiled=True)
    got = got.transpose(1, 2, 3, 0, 4).reshape(2, bc, nt, ndev * kc)
    return got[:, :, None]


def fb_transform(filtered, cos_table, sin_table):
    width = cos_table.shape[0]
    flat_re = filtered[0].reshape(-1, width)
    flat_im = filtered[1].reshape(-1, width)
    out_re = jnp.dot(flat_re, cos_table, preferred_element_type=jnp.float32) + jnp.dot(
        flat_im, sin_table, preferred_element_type=jnp.float32
    )
    out_im = jnp.dot(flat_im, cos_table, preferred_element_type=jnp.float32) - jnp.dot(
        flat_re, sin_table, preferred_element_type=jnp.float32
    )
    return jnp.stack([out_re, out_im]).astype(jnp.bfloat16).reshape(filtered.shape)


def fb_batched(matrix, vectors):
    return jnp.einsum("ksu,kub->ksb", matrix, vectors, precision=lax.Precision.HIGHEST)


def fb_iterate(rows_re, rows_im, steer_re, steer_im, diag_total, load, collect, combine):
    weight_re = steer_re / diag_total
    weight_im = steer_im / diag_total
    for sweep_no in range(2):
        full_re, full_im = collect(weight_re, weight_im)
        prod_re = fb_batched(rows_re, full_re) - fb_batched(rows_im, full_im)
        prod_im = fb_batched(rows_re, full_im) + fb_batched(rows_im, full_re)
        prod_re, prod_im = combine(prod_re, prod_im)
        next_re = weight_re + 0.5 * (steer_re - prod_re - load * weight_re) / diag_total
        next_im = weight_im + 0.5 * (steer_im - prod_im - load * weight_im) / diag_total
        weight_re, weight_im = (next_re, next_im)
    return collect(weight_re, weight_im)


def unchanged(part_re, part_im):
    return (part_re, part_im)


def fb_local(voltages, filter_coeffs, station_gain, flags, steer_index):
    cos_table, sin_table = dft_tables(filter_coeffs.shape[1])
    row_gain = station_gain * flags[0].astype(jnp.float32)
    filtered = polyphase(voltages[:, 0], filter_coeffs, row_gain)
    local_spec = fb_transform(filtered, cos_table, sin_table)
    spectra = lax.all_to_all(local_spec, "st", split_axis=3, concat_axis=1, tiled=True)
    stations = spectra.shape[1]
    chans = spectra.shape[3]
    counted = lax.axis_size("blk") * spectra.shape[2]
    spec_re = spectra[0]
    spec_im = spectra[1]
    cov_re = jnp.einsum(
        "stk,utk->ksu", spec_re, spec_re, preferred_element_type=jnp.float32
    ) + jnp.einsum("stk,utk->ksu", spec_im, spec_im, preferred_element_type=jnp.float32)
    cov_im = jnp.einsum(
        "stk,utk->ksu", spec_im, spec_re, preferred_element_type=jnp.float32
    ) - jnp.einsum("stk,utk->ksu", spec_re, spec_im, preferred_element_type=jnp.float32)
    channel_ids = lax.axis_index("st") * chans + jnp.arange(chans, dtype=jnp.int32)
    total_re, total_im = lax.psum((cov_re, cov_im), "blk")
    rows_re = total_re / counted
    rows_im = total_im / counted
    diag_part = jnp.diagonal(rows_re, axis1=1, axis2=2)
    load = jnp.sum(diag_part, axis=1) / stations + 1e-05
    phase_int = steer_index[None, :, :] * (channel_ids + 1)[:, None, None] % PHASES
    angle = phase_int.astype(jnp.float32) * (2.0 * math.pi / PHASES)
    steer_re = jnp.cos(angle)
    steer_im = jnp.sin(angle)
    load_full = load[:, None, None]
    diag_total = (diag_part + load[:, None])[:, :, None]
    weight_re, weight_im = fb_iterate(
        rows_re, rows_im, steer_re, steer_im, diag_total, load_full, unchanged, unchanged
    )
    half_re = weight_re.astype(jnp.bfloat16)
    half_im = weight_im.astype(jnp.bfloat16)
    beam_re = jnp.einsum(
        "ksb,stk->btk", half_re, spec_re, preferred_element_type=jnp.float32
    ) + jnp.einsum("ksb,stk->btk", half_im, spec_im, preferred_element_type=jnp.float32)
    beam_im = jnp.einsum(
        "ksb,stk->btk", half_re, spec_im, preferred_element_type=jnp.float32
    ) - jnp.einsum("ksb,stk->btk", half_im, spec_re, preferred_element_type=jnp.float32)
    factor = 1.0 / math.sqrt(stations)
    beam_local = (jnp.stack([beam_re, beam_im]) * factor).astype(jnp.bfloat16)
    owned = lax.all_to_all(beam_local, "st", split_axis=1, concat_axis=3, tiled=True)
    return owned[:, :, None]


def body(voltages, filter_coeffs, station_gain, flags, steer_index):
    ndev = lax.axis_size("blk") * lax.axis_size("st")
    plan = local if filter_coeffs.shape[1] % ndev == 0 else fb_local
    return plan(voltages, filter_coeffs, station_gain, flags, steer_index)


def solution(mesh):
    return jax.shard_map(
        body,
        mesh=mesh,
        in_specs=(P(None, "blk", "st", None), P(), P("st"), P("blk", "st"), P()),
        out_specs=P(None, "st", "blk", None, None),
        check_vma=False,
    )
```

```python
import math

import jax
import jax.numpy as jnp
from jax import lax
from jax.sharding import PartitionSpec as P

PHASES = 4096
AXES = ("blk", "st")


def dft_tables(width):
    counter = jnp.arange(width, dtype=jnp.int32)
    product = counter[:, None] * counter[None, :] % width
    angle = product.astype(jnp.float32) * (2.0 * math.pi / width)
    factor = 1.0 / math.sqrt(width)
    return (
        (jnp.cos(angle) * factor).astype(jnp.bfloat16),
        (jnp.sin(angle) * factor).astype(jnp.bfloat16),
    )


def polyphase(samples, filter_coeffs, row_gain):
    ntaps = filter_coeffs.shape[0]
    width = filter_coeffs.shape[1]
    grid = samples.astype(jnp.float32).reshape(2, samples.shape[1], -1, width)
    count = grid.shape[2] - ntaps + 1
    filtered = filter_coeffs[0][None, None, None, :] * grid[:, :, 0:count, :]
    for tap_no in range(1, ntaps):
        filtered = (
            filtered
            + filter_coeffs[tap_no][None, None, None, :] * grid[:, :, tap_no : tap_no + count, :]
        )
    return (filtered * row_gain[None, :, None, None]).astype(jnp.bfloat16)


def transform(filtered, cos_table, sin_table):
    flat_re = filtered[0]
    flat_im = filtered[1]
    dot = lambda a, b: jnp.einsum("stc,ck->stk", a, b, preferred_element_type=jnp.float32)
    out_re = dot(flat_re, cos_table) + dot(flat_im, sin_table)
    out_im = dot(flat_im, cos_table) - dot(flat_re, sin_table)
    return jnp.stack([out_re, out_im]).astype(jnp.bfloat16)


def batched(matrix, vectors):
    return jnp.einsum("ksu,kub->ksb", matrix, vectors, precision=lax.Precision.HIGHEST)


def iterate(rows_re, rows_im, steer_re, steer_im, diag_total, load):
    weight_re = steer_re / diag_total
    weight_im = steer_im / diag_total
    for sweep_no in range(2):
        prod_re = batched(rows_re, weight_re) - batched(rows_im, weight_im)
        prod_im = batched(rows_re, weight_im) + batched(rows_im, weight_re)
        next_re = weight_re + 0.5 * (steer_re - prod_re - load * weight_re) / diag_total
        next_im = weight_im + 0.5 * (steer_im - prod_im - load * weight_im) / diag_total
        weight_re, weight_im = (next_re, next_im)
    return weight_re, weight_im


def local(voltages, filter_coeffs, station_gain, flags, steer_index):
    nblk = lax.axis_size("blk")
    nst = lax.axis_size("st")
    ndev = nblk * nst
    cos_table, sin_table = dft_tables(filter_coeffs.shape[1])
    row_gain = station_gain * flags[0].astype(jnp.float32)
    filtered = polyphase(voltages[:, 0], filter_coeffs, row_gain)
    local_spec = transform(filtered, cos_table, sin_table)
    _, ls, nt, nk = local_spec.shape
    kc = nk // ndev
    stations = nst * ls
    counted = nblk * nt
    send = local_spec.reshape(2, ls, nt, ndev, kc).transpose(4, 3, 0, 1, 2)
    me = lax.axis_index("blk") * nst + lax.axis_index("st")
    eye = jnp.eye(stations, dtype=jnp.float32)
    factor = 1.0 / math.sqrt(stations)
    cdot = lambda a, b: jnp.einsum("st,ut->su", a, b, preferred_element_type=jnp.float32)
    bdot = lambda a, b: jnp.einsum("sb,st->bt", a, b, preferred_element_type=jnp.float32)
    got = []
    for c in range(kc):
        recv = lax.all_to_all(send[c], AXES, split_axis=0, concat_axis=0, tiled=True)
        recv = recv.reshape(nblk, nst, 2, ls, nt)
        spec = recv.transpose(2, 1, 3, 0, 4).reshape(2, stations, counted)
        spec_re = spec[0]
        spec_im = spec[1]
        rows_re = (cdot(spec_re, spec_re) + cdot(spec_im, spec_im)) / counted
        rows_im = (cdot(spec_im, spec_re) - cdot(spec_re, spec_im)) / counted
        diag_part = jnp.sum(rows_re * eye, axis=1)
        load = jnp.sum(diag_part) / stations + 1e-05
        channel_no = me * kc + c
        phase_int = steer_index * (channel_no + 1) % PHASES
        angle = phase_int.astype(jnp.float32) * (2.0 * math.pi / PHASES)
        steer_re = jnp.cos(angle)
        steer_im = jnp.sin(angle)
        diag_total = (diag_part + load)[:, None]
        weight_re, weight_im = iterate(
            rows_re[None], rows_im[None], steer_re[None], steer_im[None], diag_total[None], load
        )
        half_re = weight_re[0].astype(jnp.bfloat16)
        half_im = weight_im[0].astype(jnp.bfloat16)
        beam_re = bdot(half_re, spec_re) + bdot(half_im, spec_im)
        beam_im = bdot(half_re, spec_im) - bdot(half_im, spec_re)
        beam = (jnp.stack([beam_re, beam_im]) * factor).astype(jnp.bfloat16)
        nb = beam.shape[1]
        bc = nb // nst
        out = beam.reshape(2, nst, bc, nblk, nt).transpose(3, 1, 0, 2, 4).reshape(ndev, 2, bc, nt)
        got.append(lax.all_to_all(out, AXES, split_axis=0, concat_axis=0, tiled=True))
    res = jnp.stack(got, axis=4).transpose(1, 2, 3, 0, 4).reshape(2, bc, nt, ndev * kc)
    return res[:, :, None]


def fb_transform(filtered, cos_table, sin_table):
    width = cos_table.shape[0]
    flat_re = filtered[0].reshape(-1, width)
    flat_im = filtered[1].reshape(-1, width)
    out_re = jnp.dot(flat_re, cos_table, preferred_element_type=jnp.float32) + jnp.dot(
        flat_im, sin_table, preferred_element_type=jnp.float32
    )
    out_im = jnp.dot(flat_im, cos_table, preferred_element_type=jnp.float32) - jnp.dot(
        flat_re, sin_table, preferred_element_type=jnp.float32
    )
    return jnp.stack([out_re, out_im]).astype(jnp.bfloat16).reshape(filtered.shape)


def fb_batched(matrix, vectors):
    return jnp.einsum("ksu,kub->ksb", matrix, vectors, precision=lax.Precision.HIGHEST)


def fb_iterate(rows_re, rows_im, steer_re, steer_im, diag_total, load, collect, combine):
    weight_re = steer_re / diag_total
    weight_im = steer_im / diag_total
    for sweep_no in range(2):
        full_re, full_im = collect(weight_re, weight_im)
        prod_re = fb_batched(rows_re, full_re) - fb_batched(rows_im, full_im)
        prod_im = fb_batched(rows_re, full_im) + fb_batched(rows_im, full_re)
        prod_re, prod_im = combine(prod_re, prod_im)
        next_re = weight_re + 0.5 * (steer_re - prod_re - load * weight_re) / diag_total
        next_im = weight_im + 0.5 * (steer_im - prod_im - load * weight_im) / diag_total
        weight_re, weight_im = (next_re, next_im)
    return collect(weight_re, weight_im)


def unchanged(part_re, part_im):
    return (part_re, part_im)


def fb_local(voltages, filter_coeffs, station_gain, flags, steer_index):
    cos_table, sin_table = dft_tables(filter_coeffs.shape[1])
    row_gain = station_gain * flags[0].astype(jnp.float32)
    filtered = polyphase(voltages[:, 0], filter_coeffs, row_gain)
    local_spec = fb_transform(filtered, cos_table, sin_table)
    spectra = lax.all_to_all(local_spec, "st", split_axis=3, concat_axis=1, tiled=True)
    stations = spectra.shape[1]
    chans = spectra.shape[3]
    counted = lax.axis_size("blk") * spectra.shape[2]
    spec_re = spectra[0]
    spec_im = spectra[1]
    cov_re = jnp.einsum(
        "stk,utk->ksu", spec_re, spec_re, preferred_element_type=jnp.float32
    ) + jnp.einsum("stk,utk->ksu", spec_im, spec_im, preferred_element_type=jnp.float32)
    cov_im = jnp.einsum(
        "stk,utk->ksu", spec_im, spec_re, preferred_element_type=jnp.float32
    ) - jnp.einsum("stk,utk->ksu", spec_re, spec_im, preferred_element_type=jnp.float32)
    channel_ids = lax.axis_index("st") * chans + jnp.arange(chans, dtype=jnp.int32)
    total_re, total_im = lax.psum((cov_re, cov_im), "blk")
    rows_re = total_re / counted
    rows_im = total_im / counted
    diag_part = jnp.diagonal(rows_re, axis1=1, axis2=2)
    load = jnp.sum(diag_part, axis=1) / stations + 1e-05
    phase_int = steer_index[None, :, :] * (channel_ids + 1)[:, None, None] % PHASES
    angle = phase_int.astype(jnp.float32) * (2.0 * math.pi / PHASES)
    steer_re = jnp.cos(angle)
    steer_im = jnp.sin(angle)
    load_full = load[:, None, None]
    diag_total = (diag_part + load[:, None])[:, :, None]
    weight_re, weight_im = fb_iterate(
        rows_re, rows_im, steer_re, steer_im, diag_total, load_full, unchanged, unchanged
    )
    half_re = weight_re.astype(jnp.bfloat16)
    half_im = weight_im.astype(jnp.bfloat16)
    beam_re = jnp.einsum(
        "ksb,stk->btk", half_re, spec_re, preferred_element_type=jnp.float32
    ) + jnp.einsum("ksb,stk->btk", half_im, spec_im, preferred_element_type=jnp.float32)
    beam_im = jnp.einsum(
        "ksb,stk->btk", half_re, spec_im, preferred_element_type=jnp.float32
    ) - jnp.einsum("ksb,stk->btk", half_im, spec_re, preferred_element_type=jnp.float32)
    factor = 1.0 / math.sqrt(stations)
    beam_local = (jnp.stack([beam_re, beam_im]) * factor).astype(jnp.bfloat16)
    owned = lax.all_to_all(beam_local, "st", split_axis=1, concat_axis=3, tiled=True)
    return owned[:, :, None]


def body(voltages, filter_coeffs, station_gain, flags, steer_index):
    ndev = lax.axis_size("blk") * lax.axis_size("st")
    plan = local if filter_coeffs.shape[1] % ndev == 0 else fb_local
    return plan(voltages, filter_coeffs, station_gain, flags, steer_index)


def solution(mesh):
    return jax.shard_map(
        body,
        mesh=mesh,
        in_specs=(P(None, "blk", "st", None), P(), P("st"), P("blk", "st"), P()),
        out_specs=P(None, "st", "blk", None, None),
        check_vma=False,
    )
```

```python
import math

import jax
import jax.numpy as jnp
from jax import lax
from jax.sharding import PartitionSpec as P

PHASES = 4096
AXES = ("blk", "st")


def dft_tables(width):
    counter = jnp.arange(width, dtype=jnp.int32)
    product = counter[:, None] * counter[None, :] % width
    angle = product.astype(jnp.float32) * (2.0 * math.pi / width)
    factor = 1.0 / math.sqrt(width)
    return (
        (jnp.cos(angle) * factor).astype(jnp.bfloat16),
        (jnp.sin(angle) * factor).astype(jnp.bfloat16),
    )


def polyphase(samples, filter_coeffs, row_gain):
    ntaps = filter_coeffs.shape[0]
    width = filter_coeffs.shape[1]
    grid = samples.astype(jnp.float32).reshape(2, samples.shape[1], -1, width)
    count = grid.shape[2] - ntaps + 1
    filtered = filter_coeffs[0][None, None, None, :] * grid[:, :, 0:count, :]
    for tap_no in range(1, ntaps):
        filtered = (
            filtered
            + filter_coeffs[tap_no][None, None, None, :] * grid[:, :, tap_no : tap_no + count, :]
        )
    return (filtered * row_gain[None, :, None, None]).astype(jnp.bfloat16)


def transform(filtered, cos_table, sin_table):
    flat_re = filtered[0]
    flat_im = filtered[1]
    dot = lambda a, b: jnp.einsum("stc,ck->stk", a, b, preferred_element_type=jnp.float32)
    out_re = dot(flat_re, cos_table) + dot(flat_im, sin_table)
    out_im = dot(flat_im, cos_table) - dot(flat_re, sin_table)
    return jnp.stack([out_re, out_im]).astype(jnp.bfloat16)


def batched(matrix, vectors):
    return jnp.einsum("ksu,kub->ksb", matrix, vectors, precision=lax.Precision.HIGHEST)


def iterate(rows_re, rows_im, steer_re, steer_im, diag_total, load):
    weight_re = steer_re / diag_total
    weight_im = steer_im / diag_total
    for sweep_no in range(2):
        prod_re = batched(rows_re, weight_re) - batched(rows_im, weight_im)
        prod_im = batched(rows_re, weight_im) + batched(rows_im, weight_re)
        next_re = weight_re + 0.5 * (steer_re - prod_re - load * weight_re) / diag_total
        next_im = weight_im + 0.5 * (steer_im - prod_im - load * weight_im) / diag_total
        weight_re, weight_im = (next_re, next_im)
    return weight_re, weight_im


def local(voltages, filter_coeffs, station_gain, flags, steer_index):
    nblk = lax.axis_size("blk")
    nst = lax.axis_size("st")
    ndev = nblk * nst
    cos_table, sin_table = dft_tables(filter_coeffs.shape[1])
    row_gain = station_gain * flags[0].astype(jnp.float32)
    filtered = polyphase(voltages[:, 0], filter_coeffs, row_gain)
    local_spec = transform(filtered, cos_table, sin_table)
    _, ls, nt, nk = local_spec.shape
    kc = nk // ndev
    stations = nst * ls
    counted = nblk * nt
    send = local_spec.reshape(2, ls, nt, ndev, kc).transpose(4, 3, 0, 1, 2)
    me = lax.axis_index("blk") * nst + lax.axis_index("st")
    eye = jnp.eye(stations, dtype=jnp.float32)
    factor = 1.0 / math.sqrt(stations)
    hi = lax.Precision.HIGHEST
    got = []
    for c in range(kc):
        recv = lax.all_to_all(send[c], AXES, split_axis=0, concat_axis=0, tiled=True)
        recv = recv.reshape(nblk, nst, 2, ls, nt)
        spec = recv.transpose(2, 1, 3, 0, 4).reshape(2 * stations, counted)
        gram = jnp.dot(spec, spec.T, preferred_element_type=jnp.float32)
        g00 = gram[:stations, :stations]
        g01 = gram[:stations, stations:]
        g10 = gram[stations:, :stations]
        g11 = gram[stations:, stations:]
        rows_re = (g00 + g11) / counted
        rows_im = (g10 - g01) / counted
        rows = jnp.concatenate([rows_re, rows_im], axis=0)
        diag_part = jnp.sum(rows_re * eye, axis=1)
        load = jnp.sum(diag_part) / stations + 1e-05
        channel_no = me * kc + c
        phase_int = steer_index * (channel_no + 1) % PHASES
        angle = phase_int.astype(jnp.float32) * (2.0 * math.pi / PHASES)
        steer_re = jnp.cos(angle)
        steer_im = jnp.sin(angle)
        diag_total = (diag_part + load)[:, None]
        weight_re = steer_re / diag_total
        weight_im = steer_im / diag_total
        nb = weight_re.shape[1]
        for sweep_no in range(2):
            both = jnp.concatenate([weight_re, weight_im], axis=1)
            prod = jnp.dot(rows, both, precision=hi)
            prod_re = prod[:stations, :nb] - prod[stations:, nb:]
            prod_im = prod[:stations, nb:] + prod[stations:, :nb]
            next_re = weight_re + 0.5 * (steer_re - prod_re - load * weight_re) / diag_total
            next_im = weight_im + 0.5 * (steer_im - prod_im - load * weight_im) / diag_total
            weight_re, weight_im = (next_re, next_im)
        half_re = weight_re.astype(jnp.bfloat16)
        half_im = weight_im.astype(jnp.bfloat16)
        lhs = jnp.concatenate(
            [jnp.concatenate([half_re, -half_im], axis=1), jnp.concatenate([half_im, half_re], axis=1)],
            axis=0,
        )
        beam = jnp.dot(lhs.T, spec, preferred_element_type=jnp.float32)
        beam = (beam * factor).astype(jnp.bfloat16)
        bc = nb // nst
        out = beam.reshape(2, nst, bc, nblk, nt).transpose(3, 1, 0, 2, 4).reshape(ndev, 2, bc, nt)
        got.append(lax.all_to_all(out, AXES, split_axis=0, concat_axis=0, tiled=True))
    res = jnp.stack(got, axis=4).transpose(1, 2, 3, 0, 4).reshape(2, bc, nt, ndev * kc)
    return res[:, :, None]


def fb_transform(filtered, cos_table, sin_table):
    width = cos_table.shape[0]
    flat_re = filtered[0].reshape(-1, width)
    flat_im = filtered[1].reshape(-1, width)
    out_re = jnp.dot(flat_re, cos_table, preferred_element_type=jnp.float32) + jnp.dot(
        flat_im, sin_table, preferred_element_type=jnp.float32
    )
    out_im = jnp.dot(flat_im, cos_table, preferred_element_type=jnp.float32) - jnp.dot(
        flat_re, sin_table, preferred_element_type=jnp.float32
    )
    return jnp.stack([out_re, out_im]).astype(jnp.bfloat16).reshape(filtered.shape)


def fb_batched(matrix, vectors):
    return jnp.einsum("ksu,kub->ksb", matrix, vectors, precision=lax.Precision.HIGHEST)


def fb_iterate(rows_re, rows_im, steer_re, steer_im, diag_total, load, collect, combine):
    weight_re = steer_re / diag_total
    weight_im = steer_im / diag_total
    for sweep_no in range(2):
        full_re, full_im = collect(weight_re, weight_im)
        prod_re = fb_batched(rows_re, full_re) - fb_batched(rows_im, full_im)
        prod_im = fb_batched(rows_re, full_im) + fb_batched(rows_im, full_re)
        prod_re, prod_im = combine(prod_re, prod_im)
        next_re = weight_re + 0.5 * (steer_re - prod_re - load * weight_re) / diag_total
        next_im = weight_im + 0.5 * (steer_im - prod_im - load * weight_im) / diag_total
        weight_re, weight_im = (next_re, next_im)
    return collect(weight_re, weight_im)


def unchanged(part_re, part_im):
    return (part_re, part_im)


def fb_local(voltages, filter_coeffs, station_gain, flags, steer_index):
    cos_table, sin_table = dft_tables(filter_coeffs.shape[1])
    row_gain = station_gain * flags[0].astype(jnp.float32)
    filtered = polyphase(voltages[:, 0], filter_coeffs, row_gain)
    local_spec = fb_transform(filtered, cos_table, sin_table)
    spectra = lax.all_to_all(local_spec, "st", split_axis=3, concat_axis=1, tiled=True)
    stations = spectra.shape[1]
    chans = spectra.shape[3]
    counted = lax.axis_size("blk") * spectra.shape[2]
    spec_re = spectra[0]
    spec_im = spectra[1]
    cov_re = jnp.einsum(
        "stk,utk->ksu", spec_re, spec_re, preferred_element_type=jnp.float32
    ) + jnp.einsum("stk,utk->ksu", spec_im, spec_im, preferred_element_type=jnp.float32)
    cov_im = jnp.einsum(
        "stk,utk->ksu", spec_im, spec_re, preferred_element_type=jnp.float32
    ) - jnp.einsum("stk,utk->ksu", spec_re, spec_im, preferred_element_type=jnp.float32)
    channel_ids = lax.axis_index("st") * chans + jnp.arange(chans, dtype=jnp.int32)
    total_re, total_im = lax.psum((cov_re, cov_im), "blk")
    rows_re = total_re / counted
    rows_im = total_im / counted
    diag_part = jnp.diagonal(rows_re, axis1=1, axis2=2)
    load = jnp.sum(diag_part, axis=1) / stations + 1e-05
    phase_int = steer_index[None, :, :] * (channel_ids + 1)[:, None, None] % PHASES
    angle = phase_int.astype(jnp.float32) * (2.0 * math.pi / PHASES)
    steer_re = jnp.cos(angle)
    steer_im = jnp.sin(angle)
    load_full = load[:, None, None]
    diag_total = (diag_part + load[:, None])[:, :, None]
    weight_re, weight_im = fb_iterate(
        rows_re, rows_im, steer_re, steer_im, diag_total, load_full, unchanged, unchanged
    )
    half_re = weight_re.astype(jnp.bfloat16)
    half_im = weight_im.astype(jnp.bfloat16)
    beam_re = jnp.einsum(
        "ksb,stk->btk", half_re, spec_re, preferred_element_type=jnp.float32
    ) + jnp.einsum("ksb,stk->btk", half_im, spec_im, preferred_element_type=jnp.float32)
    beam_im = jnp.einsum(
        "ksb,stk->btk", half_re, spec_im, preferred_element_type=jnp.float32
    ) - jnp.einsum("ksb,stk->btk", half_im, spec_re, preferred_element_type=jnp.float32)
    factor = 1.0 / math.sqrt(stations)
    beam_local = (jnp.stack([beam_re, beam_im]) * factor).astype(jnp.bfloat16)
    owned = lax.all_to_all(beam_local, "st", split_axis=1, concat_axis=3, tiled=True)
    return owned[:, :, None]


def body(voltages, filter_coeffs, station_gain, flags, steer_index):
    ndev = lax.axis_size("blk") * lax.axis_size("st")
    plan = local if filter_coeffs.shape[1] % ndev == 0 else fb_local
    return plan(voltages, filter_coeffs, station_gain, flags, steer_index)


def solution(mesh):
    return jax.shard_map(
        body,
        mesh=mesh,
        in_specs=(P(None, "blk", "st", None), P(), P("st"), P("blk", "st"), P()),
        out_specs=P(None, "st", "blk", None, None),
        check_vma=False,
    )
```

```python
import math

import jax
import jax.numpy as jnp
from jax import lax
from jax.sharding import PartitionSpec as P

PHASES = 4096
AXES = ("blk", "st")


def dft_tables(width):
    counter = jnp.arange(width, dtype=jnp.int32)
    product = counter[:, None] * counter[None, :] % width
    angle = product.astype(jnp.float32) * (2.0 * math.pi / width)
    factor = 1.0 / math.sqrt(width)
    return (
        (jnp.cos(angle) * factor).astype(jnp.bfloat16),
        (jnp.sin(angle) * factor).astype(jnp.bfloat16),
    )


def polyphase(samples, filter_coeffs, row_gain):
    ntaps = filter_coeffs.shape[0]
    width = filter_coeffs.shape[1]
    grid = samples.astype(jnp.float32).reshape(2, samples.shape[1], -1, width)
    count = grid.shape[2] - ntaps + 1
    filtered = filter_coeffs[0][None, None, None, :] * grid[:, :, 0:count, :]
    for tap_no in range(1, ntaps):
        filtered = (
            filtered
            + filter_coeffs[tap_no][None, None, None, :] * grid[:, :, tap_no : tap_no + count, :]
        )
    return (filtered * row_gain[None, :, None, None]).astype(jnp.bfloat16)


def transform(filtered, cos_table, sin_table):
    flat_re = filtered[0]
    flat_im = filtered[1]
    dot = lambda a, b: jnp.einsum("stc,ck->stk", a, b, preferred_element_type=jnp.float32)
    out_re = dot(flat_re, cos_table) + dot(flat_im, sin_table)
    out_im = dot(flat_im, cos_table) - dot(flat_re, sin_table)
    return jnp.stack([out_re, out_im]).astype(jnp.bfloat16)


def batched(matrix, vectors):
    return jnp.einsum("ksu,kub->ksb", matrix, vectors, precision=lax.Precision.HIGHEST)


def iterate(rows_re, rows_im, steer_re, steer_im, diag_total, load):
    weight_re = steer_re / diag_total
    weight_im = steer_im / diag_total
    for sweep_no in range(2):
        prod_re = batched(rows_re, weight_re) - batched(rows_im, weight_im)
        prod_im = batched(rows_re, weight_im) + batched(rows_im, weight_re)
        next_re = weight_re + 0.5 * (steer_re - prod_re - load * weight_re) / diag_total
        next_im = weight_im + 0.5 * (steer_im - prod_im - load * weight_im) / diag_total
        weight_re, weight_im = (next_re, next_im)
    return weight_re, weight_im


def local(voltages, filter_coeffs, station_gain, flags, steer_index):
    nblk = lax.axis_size("blk")
    nst = lax.axis_size("st")
    ndev = nblk * nst
    ntaps, nk = filter_coeffs.shape
    cos_table, sin_table = dft_tables(nk)
    row_gain = station_gain * flags[0].astype(jnp.float32)
    samples = voltages[:, 0]
    ls = samples.shape[1]
    nt = samples.shape[2] // nk - ntaps + 1
    kc = nk // ndev
    stations = nst * ls
    counted = nblk * nt
    ngr = 4 if ls % 64 == 0 else 1
    gs = ls // ngr
    me = lax.axis_index("blk") * nst + lax.axis_index("st")
    eye = jnp.eye(stations, dtype=jnp.float32)
    factor = 1.0 / math.sqrt(stations)
    arrived = []
    for g in range(ngr):
        part = samples[:, g * gs : (g + 1) * gs]
        filtered = polyphase(part, filter_coeffs, row_gain[g * gs : (g + 1) * gs])
        local_spec = transform(filtered, cos_table, sin_table)
        send = local_spec.reshape(2, gs, nt, ndev, kc).transpose(3, 4, 0, 1, 2)
        arrived.append(lax.all_to_all(send, AXES, split_axis=0, concat_axis=0, tiled=True))
    recv_all = jnp.stack(arrived, axis=3).reshape(nblk, nst, kc, 2, ngr, gs, nt)
    hi = lax.Precision.HIGHEST
    got = []
    for c in range(kc):
        recv = recv_all[:, :, c]
        spec = recv.transpose(2, 1, 3, 4, 0, 5).reshape(2 * stations, counted)
        gram = jnp.dot(spec, spec.T, preferred_element_type=jnp.float32)
        g00 = gram[:stations, :stations]
        g01 = gram[:stations, stations:]
        g10 = gram[stations:, :stations]
        g11 = gram[stations:, stations:]
        rows_re = (g00 + g11) / counted
        rows_im = (g10 - g01) / counted
        rows = jnp.concatenate([rows_re, rows_im], axis=0)
        diag_part = jnp.sum(rows_re * eye, axis=1)
        load = jnp.sum(diag_part) / stations + 1e-05
        channel_no = me * kc + c
        phase_int = steer_index * (channel_no + 1) % PHASES
        angle = phase_int.astype(jnp.float32) * (2.0 * math.pi / PHASES)
        steer_re = jnp.cos(angle)
        steer_im = jnp.sin(angle)
        diag_total = (diag_part + load)[:, None]
        weight_re = steer_re / diag_total
        weight_im = steer_im / diag_total
        nb = weight_re.shape[1]
        for sweep_no in range(2):
            both = jnp.concatenate([weight_re, weight_im], axis=1)
            prod = jnp.dot(rows, both, precision=hi)
            prod_re = prod[:stations, :nb] - prod[stations:, nb:]
            prod_im = prod[:stations, nb:] + prod[stations:, :nb]
            next_re = weight_re + 0.5 * (steer_re - prod_re - load * weight_re) / diag_total
            next_im = weight_im + 0.5 * (steer_im - prod_im - load * weight_im) / diag_total
            weight_re, weight_im = (next_re, next_im)
        half_re = weight_re.astype(jnp.bfloat16)
        half_im = weight_im.astype(jnp.bfloat16)
        lhs = jnp.concatenate(
            [jnp.concatenate([half_re, -half_im], axis=1), jnp.concatenate([half_im, half_re], axis=1)],
            axis=0,
        )
        beam = jnp.dot(lhs.T, spec, preferred_element_type=jnp.float32)
        beam = (beam * factor).astype(jnp.bfloat16)
        bc = nb // nst
        out = beam.reshape(2, nst, bc, nblk, nt).transpose(3, 1, 0, 2, 4).reshape(ndev, 2, bc, nt)
        got.append(lax.all_to_all(out, AXES, split_axis=0, concat_axis=0, tiled=True))
    res = jnp.stack(got, axis=4).transpose(1, 2, 3, 0, 4).reshape(2, bc, nt, ndev * kc)
    return res[:, :, None]


def fb_transform(filtered, cos_table, sin_table):
    width = cos_table.shape[0]
    flat_re = filtered[0].reshape(-1, width)
    flat_im = filtered[1].reshape(-1, width)
    out_re = jnp.dot(flat_re, cos_table, preferred_element_type=jnp.float32) + jnp.dot(
        flat_im, sin_table, preferred_element_type=jnp.float32
    )
    out_im = jnp.dot(flat_im, cos_table, preferred_element_type=jnp.float32) - jnp.dot(
        flat_re, sin_table, preferred_element_type=jnp.float32
    )
    return jnp.stack([out_re, out_im]).astype(jnp.bfloat16).reshape(filtered.shape)


def fb_batched(matrix, vectors):
    return jnp.einsum("ksu,kub->ksb", matrix, vectors, precision=lax.Precision.HIGHEST)


def fb_iterate(rows_re, rows_im, steer_re, steer_im, diag_total, load, collect, combine):
    weight_re = steer_re / diag_total
    weight_im = steer_im / diag_total
    for sweep_no in range(2):
        full_re, full_im = collect(weight_re, weight_im)
        prod_re = fb_batched(rows_re, full_re) - fb_batched(rows_im, full_im)
        prod_im = fb_batched(rows_re, full_im) + fb_batched(rows_im, full_re)
        prod_re, prod_im = combine(prod_re, prod_im)
        next_re = weight_re + 0.5 * (steer_re - prod_re - load * weight_re) / diag_total
        next_im = weight_im + 0.5 * (steer_im - prod_im - load * weight_im) / diag_total
        weight_re, weight_im = (next_re, next_im)
    return collect(weight_re, weight_im)


def unchanged(part_re, part_im):
    return (part_re, part_im)


def fb_local(voltages, filter_coeffs, station_gain, flags, steer_index):
    cos_table, sin_table = dft_tables(filter_coeffs.shape[1])
    row_gain = station_gain * flags[0].astype(jnp.float32)
    filtered = polyphase(voltages[:, 0], filter_coeffs, row_gain)
    local_spec = fb_transform(filtered, cos_table, sin_table)
    spectra = lax.all_to_all(local_spec, "st", split_axis=3, concat_axis=1, tiled=True)
    stations = spectra.shape[1]
    chans = spectra.shape[3]
    counted = lax.axis_size("blk") * spectra.shape[2]
    spec_re = spectra[0]
    spec_im = spectra[1]
    cov_re = jnp.einsum(
        "stk,utk->ksu", spec_re, spec_re, preferred_element_type=jnp.float32
    ) + jnp.einsum("stk,utk->ksu", spec_im, spec_im, preferred_element_type=jnp.float32)
    cov_im = jnp.einsum(
        "stk,utk->ksu", spec_im, spec_re, preferred_element_type=jnp.float32
    ) - jnp.einsum("stk,utk->ksu", spec_re, spec_im, preferred_element_type=jnp.float32)
    channel_ids = lax.axis_index("st") * chans + jnp.arange(chans, dtype=jnp.int32)
    total_re, total_im = lax.psum((cov_re, cov_im), "blk")
    rows_re = total_re / counted
    rows_im = total_im / counted
    diag_part = jnp.diagonal(rows_re, axis1=1, axis2=2)
    load = jnp.sum(diag_part, axis=1) / stations + 1e-05
    phase_int = steer_index[None, :, :] * (channel_ids + 1)[:, None, None] % PHASES
    angle = phase_int.astype(jnp.float32) * (2.0 * math.pi / PHASES)
    steer_re = jnp.cos(angle)
    steer_im = jnp.sin(angle)
    load_full = load[:, None, None]
    diag_total = (diag_part + load[:, None])[:, :, None]
    weight_re, weight_im = fb_iterate(
        rows_re, rows_im, steer_re, steer_im, diag_total, load_full, unchanged, unchanged
    )
    half_re = weight_re.astype(jnp.bfloat16)
    half_im = weight_im.astype(jnp.bfloat16)
    beam_re = jnp.einsum(
        "ksb,stk->btk", half_re, spec_re, preferred_element_type=jnp.float32
    ) + jnp.einsum("ksb,stk->btk", half_im, spec_im, preferred_element_type=jnp.float32)
    beam_im = jnp.einsum(
        "ksb,stk->btk", half_re, spec_im, preferred_element_type=jnp.float32
    ) - jnp.einsum("ksb,stk->btk", half_im, spec_re, preferred_element_type=jnp.float32)
    factor = 1.0 / math.sqrt(stations)
    beam_local = (jnp.stack([beam_re, beam_im]) * factor).astype(jnp.bfloat16)
    owned = lax.all_to_all(beam_local, "st", split_axis=1, concat_axis=3, tiled=True)
    return owned[:, :, None]


def body(voltages, filter_coeffs, station_gain, flags, steer_index):
    ndev = lax.axis_size("blk") * lax.axis_size("st")
    plan = local if filter_coeffs.shape[1] % ndev == 0 else fb_local
    return plan(voltages, filter_coeffs, station_gain, flags, steer_index)


def solution(mesh):
    return jax.shard_map(
        body,
        mesh=mesh,
        in_specs=(P(None, "blk", "st", None), P(), P("st"), P("blk", "st"), P()),
        out_specs=P(None, "st", "blk", None, None),
        check_vma=False,
    )
```

```python
import math

import jax
import jax.numpy as jnp
from jax import lax
from jax.sharding import PartitionSpec as P

PHASES = 4096
AXES = ("blk", "st")


def dft_tables(width):
    counter = jnp.arange(width, dtype=jnp.int32)
    product = counter[:, None] * counter[None, :] % width
    angle = product.astype(jnp.float32) * (2.0 * math.pi / width)
    factor = 1.0 / math.sqrt(width)
    return (
        (jnp.cos(angle) * factor).astype(jnp.bfloat16),
        (jnp.sin(angle) * factor).astype(jnp.bfloat16),
    )


def polyphase(samples, filter_coeffs, row_gain):
    ntaps = filter_coeffs.shape[0]
    width = filter_coeffs.shape[1]
    grid = samples.astype(jnp.float32).reshape(2, samples.shape[1], -1, width)
    count = grid.shape[2] - ntaps + 1
    filtered = filter_coeffs[0][None, None, None, :] * grid[:, :, 0:count, :]
    for tap_no in range(1, ntaps):
        filtered = (
            filtered
            + filter_coeffs[tap_no][None, None, None, :] * grid[:, :, tap_no : tap_no + count, :]
        )
    return (filtered * row_gain[None, :, None, None]).astype(jnp.bfloat16)


def transform(filtered, cos_table, sin_table):
    flat_re = filtered[0]
    flat_im = filtered[1]
    dot = lambda a, b: jnp.einsum("stc,ck->stk", a, b, preferred_element_type=jnp.float32)
    out_re = dot(flat_re, cos_table) + dot(flat_im, sin_table)
    out_im = dot(flat_im, cos_table) - dot(flat_re, sin_table)
    return jnp.stack([out_re, out_im]).astype(jnp.bfloat16)


def batched(matrix, vectors):
    return jnp.einsum("ksu,kub->ksb", matrix, vectors, precision=lax.Precision.HIGHEST)


def iterate(rows_re, rows_im, steer_re, steer_im, diag_total, load):
    weight_re = steer_re / diag_total
    weight_im = steer_im / diag_total
    for sweep_no in range(2):
        prod_re = batched(rows_re, weight_re) - batched(rows_im, weight_im)
        prod_im = batched(rows_re, weight_im) + batched(rows_im, weight_re)
        next_re = weight_re + 0.5 * (steer_re - prod_re - load * weight_re) / diag_total
        next_im = weight_im + 0.5 * (steer_im - prod_im - load * weight_im) / diag_total
        weight_re, weight_im = (next_re, next_im)
    return weight_re, weight_im


def local(voltages, filter_coeffs, station_gain, flags, steer_index):
    nblk = lax.axis_size("blk")
    nst = lax.axis_size("st")
    ndev = nblk * nst
    ntaps, nk = filter_coeffs.shape
    cos_table, sin_table = dft_tables(nk)
    row_gain = station_gain * flags[0].astype(jnp.float32)
    samples = voltages[:, 0]
    ls = samples.shape[1]
    nt = samples.shape[2] // nk - ntaps + 1
    kc = nk // ndev
    stations = nst * ls
    counted = nblk * nt
    ngr = 4 if ls % 64 == 0 else 1
    gs = ls // ngr
    me = lax.axis_index("blk") * nst + lax.axis_index("st")
    eye = jnp.eye(stations, dtype=jnp.float32)
    factor = 1.0 / math.sqrt(stations)
    arrived = []
    for g in range(ngr):
        part = samples[:, g * gs : (g + 1) * gs]
        filtered = polyphase(part, filter_coeffs, row_gain[g * gs : (g + 1) * gs])
        local_spec = transform(filtered, cos_table, sin_table)
        send = local_spec.reshape(2, gs, nt, ndev, kc).transpose(3, 4, 0, 1, 2)
        if g < ngr - 1:
            arrived.append(lax.all_to_all(send, AXES, split_axis=0, concat_axis=0, tiled=True))
        else:
            last = [
                lax.all_to_all(send[:, c], AXES, split_axis=0, concat_axis=0, tiled=True)
                for c in range(kc)
            ]
    hi = lax.Precision.HIGHEST
    got = []
    for c in range(kc):
        pieces = [part[:, c] for part in arrived] + [last[c]]
        recv = jnp.stack(pieces, axis=2).reshape(nblk, nst, 2, ngr, gs, nt)
        spec = recv.transpose(2, 1, 3, 4, 0, 5).reshape(2 * stations, counted)
        gram = jnp.dot(spec, spec.T, preferred_element_type=jnp.float32)
        g00 = gram[:stations, :stations]
        g01 = gram[:stations, stations:]
        g10 = gram[stations:, :stations]
        g11 = gram[stations:, stations:]
        rows_re = (g00 + g11) / counted
        rows_im = (g10 - g01) / counted
        rows = jnp.concatenate([rows_re, rows_im], axis=0)
        diag_part = jnp.sum(rows_re * eye, axis=1)
        load = jnp.sum(diag_part) / stations + 1e-05
        channel_no = me * kc + c
        phase_int = steer_index * (channel_no + 1) % PHASES
        angle = phase_int.astype(jnp.float32) * (2.0 * math.pi / PHASES)
        steer_re = jnp.cos(angle)
        steer_im = jnp.sin(angle)
        diag_total = (diag_part + load)[:, None]
        weight_re = steer_re / diag_total
        weight_im = steer_im / diag_total
        nb = weight_re.shape[1]
        for sweep_no in range(2):
            both = jnp.concatenate([weight_re, weight_im], axis=1)
            prod = jnp.dot(rows, both, precision=hi)
            prod_re = prod[:stations, :nb] - prod[stations:, nb:]
            prod_im = prod[:stations, nb:] + prod[stations:, :nb]
            next_re = weight_re + 0.5 * (steer_re - prod_re - load * weight_re) / diag_total
            next_im = weight_im + 0.5 * (steer_im - prod_im - load * weight_im) / diag_total
            weight_re, weight_im = (next_re, next_im)
        half_re = weight_re.astype(jnp.bfloat16)
        half_im = weight_im.astype(jnp.bfloat16)
        lhs = jnp.concatenate(
            [jnp.concatenate([half_re, -half_im], axis=1), jnp.concatenate([half_im, half_re], axis=1)],
            axis=0,
        )
        beam = jnp.dot(lhs.T, spec, preferred_element_type=jnp.float32)
        beam = (beam * factor).astype(jnp.bfloat16)
        bc = nb // nst
        out = beam.reshape(2, nst, bc, nblk, nt).transpose(3, 1, 0, 2, 4).reshape(ndev, 2, bc, nt)
        got.append(lax.all_to_all(out, AXES, split_axis=0, concat_axis=0, tiled=True))
    res = jnp.stack(got, axis=4).transpose(1, 2, 3, 0, 4).reshape(2, bc, nt, ndev * kc)
    return res[:, :, None]


def fb_transform(filtered, cos_table, sin_table):
    width = cos_table.shape[0]
    flat_re = filtered[0].reshape(-1, width)
    flat_im = filtered[1].reshape(-1, width)
    out_re = jnp.dot(flat_re, cos_table, preferred_element_type=jnp.float32) + jnp.dot(
        flat_im, sin_table, preferred_element_type=jnp.float32
    )
    out_im = jnp.dot(flat_im, cos_table, preferred_element_type=jnp.float32) - jnp.dot(
        flat_re, sin_table, preferred_element_type=jnp.float32
    )
    return jnp.stack([out_re, out_im]).astype(jnp.bfloat16).reshape(filtered.shape)


def fb_batched(matrix, vectors):
    return jnp.einsum("ksu,kub->ksb", matrix, vectors, precision=lax.Precision.HIGHEST)


def fb_iterate(rows_re, rows_im, steer_re, steer_im, diag_total, load, collect, combine):
    weight_re = steer_re / diag_total
    weight_im = steer_im / diag_total
    for sweep_no in range(2):
        full_re, full_im = collect(weight_re, weight_im)
        prod_re = fb_batched(rows_re, full_re) - fb_batched(rows_im, full_im)
        prod_im = fb_batched(rows_re, full_im) + fb_batched(rows_im, full_re)
        prod_re, prod_im = combine(prod_re, prod_im)
        next_re = weight_re + 0.5 * (steer_re - prod_re - load * weight_re) / diag_total
        next_im = weight_im + 0.5 * (steer_im - prod_im - load * weight_im) / diag_total
        weight_re, weight_im = (next_re, next_im)
    return collect(weight_re, weight_im)


def unchanged(part_re, part_im):
    return (part_re, part_im)


def fb_local(voltages, filter_coeffs, station_gain, flags, steer_index):
    cos_table, sin_table = dft_tables(filter_coeffs.shape[1])
    row_gain = station_gain * flags[0].astype(jnp.float32)
    filtered = polyphase(voltages[:, 0], filter_coeffs, row_gain)
    local_spec = fb_transform(filtered, cos_table, sin_table)
    spectra = lax.all_to_all(local_spec, "st", split_axis=3, concat_axis=1, tiled=True)
    stations = spectra.shape[1]
    chans = spectra.shape[3]
    counted = lax.axis_size("blk") * spectra.shape[2]
    spec_re = spectra[0]
    spec_im = spectra[1]
    cov_re = jnp.einsum(
        "stk,utk->ksu", spec_re, spec_re, preferred_element_type=jnp.float32
    ) + jnp.einsum("stk,utk->ksu", spec_im, spec_im, preferred_element_type=jnp.float32)
    cov_im = jnp.einsum(
        "stk,utk->ksu", spec_im, spec_re, preferred_element_type=jnp.float32
    ) - jnp.einsum("stk,utk->ksu", spec_re, spec_im, preferred_element_type=jnp.float32)
    channel_ids = lax.axis_index("st") * chans + jnp.arange(chans, dtype=jnp.int32)
    total_re, total_im = lax.psum((cov_re, cov_im), "blk")
    rows_re = total_re / counted
    rows_im = total_im / counted
    diag_part = jnp.diagonal(rows_re, axis1=1, axis2=2)
    load = jnp.sum(diag_part, axis=1) / stations + 1e-05
    phase_int = steer_index[None, :, :] * (channel_ids + 1)[:, None, None] % PHASES
    angle = phase_int.astype(jnp.float32) * (2.0 * math.pi / PHASES)
    steer_re = jnp.cos(angle)
    steer_im = jnp.sin(angle)
    load_full = load[:, None, None]
    diag_total = (diag_part + load[:, None])[:, :, None]
    weight_re, weight_im = fb_iterate(
        rows_re, rows_im, steer_re, steer_im, diag_total, load_full, unchanged, unchanged
    )
    half_re = weight_re.astype(jnp.bfloat16)
    half_im = weight_im.astype(jnp.bfloat16)
    beam_re = jnp.einsum(
        "ksb,stk->btk", half_re, spec_re, preferred_element_type=jnp.float32
    ) + jnp.einsum("ksb,stk->btk", half_im, spec_im, preferred_element_type=jnp.float32)
    beam_im = jnp.einsum(
        "ksb,stk->btk", half_re, spec_im, preferred_element_type=jnp.float32
    ) - jnp.einsum("ksb,stk->btk", half_im, spec_re, preferred_element_type=jnp.float32)
    factor = 1.0 / math.sqrt(stations)
    beam_local = (jnp.stack([beam_re, beam_im]) * factor).astype(jnp.bfloat16)
    owned = lax.all_to_all(beam_local, "st", split_axis=1, concat_axis=3, tiled=True)
    return owned[:, :, None]


def body(voltages, filter_coeffs, station_gain, flags, steer_index):
    ndev = lax.axis_size("blk") * lax.axis_size("st")
    plan = local if filter_coeffs.shape[1] % ndev == 0 else fb_local
    return plan(voltages, filter_coeffs, station_gain, flags, steer_index)


def solution(mesh):
    return jax.shard_map(
        body,
        mesh=mesh,
        in_specs=(P(None, "blk", "st", None), P(), P("st"), P("blk", "st"), P()),
        out_specs=P(None, "st", "blk", None, None),
        check_vma=False,
    )
```

```python
import math

import jax
import jax.numpy as jnp
from jax import lax
from jax.sharding import PartitionSpec as P

PHASES = 4096
AXES = ("blk", "st")


def dft_tables(width):
    counter = jnp.arange(width, dtype=jnp.int32)
    product = counter[:, None] * counter[None, :] % width
    angle = product.astype(jnp.float32) * (2.0 * math.pi / width)
    factor = 1.0 / math.sqrt(width)
    return (
        (jnp.cos(angle) * factor).astype(jnp.bfloat16),
        (jnp.sin(angle) * factor).astype(jnp.bfloat16),
    )


def polyphase(samples, filter_coeffs, row_gain):
    ntaps = filter_coeffs.shape[0]
    width = filter_coeffs.shape[1]
    grid = samples.astype(jnp.float32).reshape(2, samples.shape[1], -1, width)
    count = grid.shape[2] - ntaps + 1
    filtered = filter_coeffs[0][None, None, None, :] * grid[:, :, 0:count, :]
    for tap_no in range(1, ntaps):
        filtered = (
            filtered
            + filter_coeffs[tap_no][None, None, None, :] * grid[:, :, tap_no : tap_no + count, :]
        )
    return (filtered * row_gain[None, :, None, None]).astype(jnp.bfloat16)


def transform(filtered, cos_table, sin_table):
    flat_re = filtered[0]
    flat_im = filtered[1]
    dot = lambda a, b: jnp.einsum("stc,ck->stk", a, b, preferred_element_type=jnp.float32)
    out_re = dot(flat_re, cos_table) + dot(flat_im, sin_table)
    out_im = dot(flat_im, cos_table) - dot(flat_re, sin_table)
    return jnp.stack([out_re, out_im]).astype(jnp.bfloat16)


def batched(matrix, vectors):
    return jnp.einsum("ksu,kub->ksb", matrix, vectors, precision=lax.Precision.HIGHEST)


def iterate(rows_re, rows_im, steer_re, steer_im, diag_total, load):
    weight_re = steer_re / diag_total
    weight_im = steer_im / diag_total
    for sweep_no in range(2):
        prod_re = batched(rows_re, weight_re) - batched(rows_im, weight_im)
        prod_im = batched(rows_re, weight_im) + batched(rows_im, weight_re)
        next_re = weight_re + 0.5 * (steer_re - prod_re - load * weight_re) / diag_total
        next_im = weight_im + 0.5 * (steer_im - prod_im - load * weight_im) / diag_total
        weight_re, weight_im = (next_re, next_im)
    return weight_re, weight_im


def local(voltages, filter_coeffs, station_gain, flags, steer_index):
    nblk = lax.axis_size("blk")
    nst = lax.axis_size("st")
    ndev = nblk * nst
    ntaps, nk = filter_coeffs.shape
    cos_table, sin_table = dft_tables(nk)
    row_gain = station_gain * flags[0].astype(jnp.float32)
    samples = voltages[:, 0]
    ls = samples.shape[1]
    nt = samples.shape[2] // nk - ntaps + 1
    kc = nk // ndev
    stations = nst * ls
    counted = nblk * nt
    ngr = 4 if ls % 64 == 0 else 1
    gs = ls // ngr
    me = lax.axis_index("blk") * nst + lax.axis_index("st")
    eye = jnp.eye(stations, dtype=jnp.float32)
    factor = 1.0 / math.sqrt(stations)
    arrived = []
    for g in range(ngr):
        part = samples[:, g * gs : (g + 1) * gs]
        filtered = polyphase(part, filter_coeffs, row_gain[g * gs : (g + 1) * gs])
        local_spec = transform(filtered, cos_table, sin_table)
        send = local_spec.reshape(2, gs, nt, ndev, kc).transpose(3, 4, 0, 1, 2)
        if g < ngr - 1:
            arrived.append(lax.all_to_all(send, AXES, split_axis=0, concat_axis=0, tiled=True))
        else:
            last = [
                lax.all_to_all(send[:, c], AXES, split_axis=0, concat_axis=0, tiled=True)
                for c in range(kc)
            ]
    hi = lax.Precision.HIGHEST
    got = []
    prev = None
    for c in range(kc):
        pieces = [part[:, c] for part in arrived] + [last[c]]
        if prev is not None:
            pieces, _ = lax.optimization_barrier((pieces, prev))
        recv = jnp.stack(pieces, axis=2).reshape(nblk, nst, 2, ngr, gs, nt)
        spec = recv.transpose(2, 1, 3, 4, 0, 5).reshape(2 * stations, counted)
        gram = jnp.dot(spec, spec.T, preferred_element_type=jnp.float32)
        g00 = gram[:stations, :stations]
        g01 = gram[:stations, stations:]
        g10 = gram[stations:, :stations]
        g11 = gram[stations:, stations:]
        rows_re = (g00 + g11) / counted
        rows_im = (g10 - g01) / counted
        rows = jnp.concatenate([rows_re, rows_im], axis=0)
        diag_part = jnp.sum(rows_re * eye, axis=1)
        load = jnp.sum(diag_part) / stations + 1e-05
        channel_no = me * kc + c
        phase_int = steer_index * (channel_no + 1) % PHASES
        angle = phase_int.astype(jnp.float32) * (2.0 * math.pi / PHASES)
        steer_re = jnp.cos(angle)
        steer_im = jnp.sin(angle)
        diag_total = (diag_part + load)[:, None]
        weight_re = steer_re / diag_total
        weight_im = steer_im / diag_total
        nb = weight_re.shape[1]
        for sweep_no in range(2):
            both = jnp.concatenate([weight_re, weight_im], axis=1)
            prod = jnp.dot(rows, both, precision=hi)
            prod_re = prod[:stations, :nb] - prod[stations:, nb:]
            prod_im = prod[:stations, nb:] + prod[stations:, :nb]
            next_re = weight_re + 0.5 * (steer_re - prod_re - load * weight_re) / diag_total
            next_im = weight_im + 0.5 * (steer_im - prod_im - load * weight_im) / diag_total
            weight_re, weight_im = (next_re, next_im)
        half_re = weight_re.astype(jnp.bfloat16)
        half_im = weight_im.astype(jnp.bfloat16)
        lhs = jnp.concatenate(
            [jnp.concatenate([half_re, -half_im], axis=1), jnp.concatenate([half_im, half_re], axis=1)],
            axis=0,
        )
        beam = jnp.dot(lhs.T, spec, preferred_element_type=jnp.float32)
        beam = (beam * factor).astype(jnp.bfloat16)
        bc = nb // nst
        out = beam.reshape(2, nst, bc, nblk, nt).transpose(3, 1, 0, 2, 4).reshape(ndev, 2, bc, nt)
        prev = out
        got.append(lax.all_to_all(out, AXES, split_axis=0, concat_axis=0, tiled=True))
    res = jnp.stack(got, axis=4).transpose(1, 2, 3, 0, 4).reshape(2, bc, nt, ndev * kc)
    return res[:, :, None]


def fb_transform(filtered, cos_table, sin_table):
    width = cos_table.shape[0]
    flat_re = filtered[0].reshape(-1, width)
    flat_im = filtered[1].reshape(-1, width)
    out_re = jnp.dot(flat_re, cos_table, preferred_element_type=jnp.float32) + jnp.dot(
        flat_im, sin_table, preferred_element_type=jnp.float32
    )
    out_im = jnp.dot(flat_im, cos_table, preferred_element_type=jnp.float32) - jnp.dot(
        flat_re, sin_table, preferred_element_type=jnp.float32
    )
    return jnp.stack([out_re, out_im]).astype(jnp.bfloat16).reshape(filtered.shape)


def fb_batched(matrix, vectors):
    return jnp.einsum("ksu,kub->ksb", matrix, vectors, precision=lax.Precision.HIGHEST)


def fb_iterate(rows_re, rows_im, steer_re, steer_im, diag_total, load, collect, combine):
    weight_re = steer_re / diag_total
    weight_im = steer_im / diag_total
    for sweep_no in range(2):
        full_re, full_im = collect(weight_re, weight_im)
        prod_re = fb_batched(rows_re, full_re) - fb_batched(rows_im, full_im)
        prod_im = fb_batched(rows_re, full_im) + fb_batched(rows_im, full_re)
        prod_re, prod_im = combine(prod_re, prod_im)
        next_re = weight_re + 0.5 * (steer_re - prod_re - load * weight_re) / diag_total
        next_im = weight_im + 0.5 * (steer_im - prod_im - load * weight_im) / diag_total
        weight_re, weight_im = (next_re, next_im)
    return collect(weight_re, weight_im)


def unchanged(part_re, part_im):
    return (part_re, part_im)


def fb_local(voltages, filter_coeffs, station_gain, flags, steer_index):
    cos_table, sin_table = dft_tables(filter_coeffs.shape[1])
    row_gain = station_gain * flags[0].astype(jnp.float32)
    filtered = polyphase(voltages[:, 0], filter_coeffs, row_gain)
    local_spec = fb_transform(filtered, cos_table, sin_table)
    spectra = lax.all_to_all(local_spec, "st", split_axis=3, concat_axis=1, tiled=True)
    stations = spectra.shape[1]
    chans = spectra.shape[3]
    counted = lax.axis_size("blk") * spectra.shape[2]
    spec_re = spectra[0]
    spec_im = spectra[1]
    cov_re = jnp.einsum(
        "stk,utk->ksu", spec_re, spec_re, preferred_element_type=jnp.float32
    ) + jnp.einsum("stk,utk->ksu", spec_im, spec_im, preferred_element_type=jnp.float32)
    cov_im = jnp.einsum(
        "stk,utk->ksu", spec_im, spec_re, preferred_element_type=jnp.float32
    ) - jnp.einsum("stk,utk->ksu", spec_re, spec_im, preferred_element_type=jnp.float32)
    channel_ids = lax.axis_index("st") * chans + jnp.arange(chans, dtype=jnp.int32)
    total_re, total_im = lax.psum((cov_re, cov_im), "blk")
    rows_re = total_re / counted
    rows_im = total_im / counted
    diag_part = jnp.diagonal(rows_re, axis1=1, axis2=2)
    load = jnp.sum(diag_part, axis=1) / stations + 1e-05
    phase_int = steer_index[None, :, :] * (channel_ids + 1)[:, None, None] % PHASES
    angle = phase_int.astype(jnp.float32) * (2.0 * math.pi / PHASES)
    steer_re = jnp.cos(angle)
    steer_im = jnp.sin(angle)
    load_full = load[:, None, None]
    diag_total = (diag_part + load[:, None])[:, :, None]
    weight_re, weight_im = fb_iterate(
        rows_re, rows_im, steer_re, steer_im, diag_total, load_full, unchanged, unchanged
    )
    half_re = weight_re.astype(jnp.bfloat16)
    half_im = weight_im.astype(jnp.bfloat16)
    beam_re = jnp.einsum(
        "ksb,stk->btk", half_re, spec_re, preferred_element_type=jnp.float32
    ) + jnp.einsum("ksb,stk->btk", half_im, spec_im, preferred_element_type=jnp.float32)
    beam_im = jnp.einsum(
        "ksb,stk->btk", half_re, spec_im, preferred_element_type=jnp.float32
    ) - jnp.einsum("ksb,stk->btk", half_im, spec_re, preferred_element_type=jnp.float32)
    factor = 1.0 / math.sqrt(stations)
    beam_local = (jnp.stack([beam_re, beam_im]) * factor).astype(jnp.bfloat16)
    owned = lax.all_to_all(beam_local, "st", split_axis=1, concat_axis=3, tiled=True)
    return owned[:, :, None]


def body(voltages, filter_coeffs, station_gain, flags, steer_index):
    ndev = lax.axis_size("blk") * lax.axis_size("st")
    plan = local if filter_coeffs.shape[1] % ndev == 0 else fb_local
    return plan(voltages, filter_coeffs, station_gain, flags, steer_index)


def solution(mesh):
    return jax.shard_map(
        body,
        mesh=mesh,
        in_specs=(P(None, "blk", "st", None), P(), P("st"), P("blk", "st"), P()),
        out_specs=P(None, "st", "blk", None, None),
        check_vma=False,
    )
```

```python
import math

import jax
import jax.numpy as jnp
from jax import lax
from jax.sharding import PartitionSpec as P

PHASES = 4096
AXES = ("blk", "st")


def dft_tables(width):
    counter = jnp.arange(width, dtype=jnp.int32)
    product = counter[:, None] * counter[None, :] % width
    angle = product.astype(jnp.float32) * (2.0 * math.pi / width)
    factor = 1.0 / math.sqrt(width)
    return (
        (jnp.cos(angle) * factor).astype(jnp.bfloat16),
        (jnp.sin(angle) * factor).astype(jnp.bfloat16),
    )


def polyphase(samples, filter_coeffs, row_gain):
    ntaps = filter_coeffs.shape[0]
    width = filter_coeffs.shape[1]
    grid = samples.astype(jnp.float32).reshape(2, samples.shape[1], -1, width)
    count = grid.shape[2] - ntaps + 1
    filtered = filter_coeffs[0][None, None, None, :] * grid[:, :, 0:count, :]
    for tap_no in range(1, ntaps):
        filtered = (
            filtered
            + filter_coeffs[tap_no][None, None, None, :] * grid[:, :, tap_no : tap_no + count, :]
        )
    return (filtered * row_gain[None, :, None, None]).astype(jnp.bfloat16)


def transform(filtered, cos_table, sin_table):
    flat_re = filtered[0]
    flat_im = filtered[1]
    dot = lambda a, b: jnp.einsum("stc,ck->stk", a, b, preferred_element_type=jnp.float32)
    out_re = dot(flat_re, cos_table) + dot(flat_im, sin_table)
    out_im = dot(flat_im, cos_table) - dot(flat_re, sin_table)
    return jnp.stack([out_re, out_im]).astype(jnp.bfloat16)


def batched(matrix, vectors):
    return jnp.einsum("ksu,kub->ksb", matrix, vectors, precision=lax.Precision.HIGHEST)


def iterate(rows_re, rows_im, steer_re, steer_im, diag_total, load):
    weight_re = steer_re / diag_total
    weight_im = steer_im / diag_total
    for sweep_no in range(2):
        prod_re = batched(rows_re, weight_re) - batched(rows_im, weight_im)
        prod_im = batched(rows_re, weight_im) + batched(rows_im, weight_re)
        next_re = weight_re + 0.5 * (steer_re - prod_re - load * weight_re) / diag_total
        next_im = weight_im + 0.5 * (steer_im - prod_im - load * weight_im) / diag_total
        weight_re, weight_im = (next_re, next_im)
    return weight_re, weight_im


def local(voltages, filter_coeffs, station_gain, flags, steer_index):
    nblk = lax.axis_size("blk")
    nst = lax.axis_size("st")
    ndev = nblk * nst
    ntaps, nk = filter_coeffs.shape
    cos_table, sin_table = dft_tables(nk)
    row_gain = station_gain * flags[0].astype(jnp.float32)
    samples = voltages[:, 0]
    ls = samples.shape[1]
    nt = samples.shape[2] // nk - ntaps + 1
    kc = nk // ndev
    stations = nst * ls
    counted = nblk * nt
    ngr = 4 if ls % 64 == 0 else 1
    gs = ls // ngr
    me = lax.axis_index("blk") * nst + lax.axis_index("st")
    eye = jnp.eye(stations, dtype=jnp.float32)
    factor = 1.0 / math.sqrt(stations)
    arrived = []
    for g in range(ngr):
        part = samples[:, g * gs : (g + 1) * gs]
        filtered = polyphase(part, filter_coeffs, row_gain[g * gs : (g + 1) * gs])
        local_spec = transform(filtered, cos_table, sin_table)
        send = local_spec.reshape(2, gs, nt, ndev, kc).transpose(3, 4, 0, 1, 2)
        if g < ngr - 1:
            arrived.append(lax.all_to_all(send, AXES, split_axis=0, concat_axis=0, tiled=True))
        else:
            last = [
                lax.all_to_all(send[:, c], AXES, split_axis=0, concat_axis=0, tiled=True)
                for c in range(kc)
            ]
    hi = lax.Precision.HIGHEST
    got = []
    prev = None
    for c in range(kc):
        pieces = [part[:, c] for part in arrived] + [last[c]]
        if prev is not None:
            pieces, _ = lax.optimization_barrier((pieces, prev))
        recv = jnp.stack(pieces, axis=2).reshape(nblk, nst, 2, ngr, gs, nt)
        spec = recv.transpose(2, 1, 3, 4, 0, 5).reshape(2 * stations, counted)
        gram = jnp.dot(spec, spec.T, preferred_element_type=jnp.float32)
        g00 = gram[:stations, :stations]
        g01 = gram[:stations, stations:]
        g10 = gram[stations:, :stations]
        g11 = gram[stations:, stations:]
        rows_re = (g00 + g11) / counted
        rows_im = (g10 - g01) / counted
        rows = jnp.concatenate([rows_re, rows_im], axis=0)
        diag_part = jnp.sum(rows_re * eye, axis=1)
        load = jnp.sum(diag_part) / stations + 1e-05
        channel_no = me * kc + c
        phase_int = steer_index * (channel_no + 1) % PHASES
        angle = phase_int.astype(jnp.float32) * (2.0 * math.pi / PHASES)
        steer_re = jnp.cos(angle)
        steer_im = jnp.sin(angle)
        diag_total = (diag_part + load)[:, None]
        weight_re = steer_re / diag_total
        weight_im = steer_im / diag_total
        nb = weight_re.shape[1]
        for sweep_no in range(2):
            both = jnp.concatenate([weight_re, weight_im], axis=1)
            prod = jnp.dot(rows, both, precision=hi)
            prod_re = prod[:stations, :nb] - prod[stations:, nb:]
            prod_im = prod[:stations, nb:] + prod[stations:, :nb]
            next_re = weight_re + 0.5 * (steer_re - prod_re - load * weight_re) / diag_total
            next_im = weight_im + 0.5 * (steer_im - prod_im - load * weight_im) / diag_total
            weight_re, weight_im = (next_re, next_im)
        half_re = weight_re.astype(jnp.bfloat16)
        half_im = weight_im.astype(jnp.bfloat16)
        lhs = jnp.concatenate(
            [jnp.concatenate([half_re, -half_im], axis=1), jnp.concatenate([half_im, half_re], axis=1)],
            axis=0,
        )
        beam = jnp.dot(lhs.T, spec, preferred_element_type=jnp.float32)
        beam = (beam * factor).astype(jnp.bfloat16)
        bc = nb // nst
        out = beam.reshape(2, nst, bc, nblk, nt).transpose(3, 1, 0, 2, 4).reshape(ndev, 2, bc, nt)
        prev = out
        got.append(out)
    sent = lax.all_to_all(jnp.stack(got, axis=1), AXES, split_axis=0, concat_axis=0, tiled=True)
    res = sent.transpose(2, 3, 4, 0, 1).reshape(2, bc, nt, ndev * kc)
    return res[:, :, None]


def fb_transform(filtered, cos_table, sin_table):
    width = cos_table.shape[0]
    flat_re = filtered[0].reshape(-1, width)
    flat_im = filtered[1].reshape(-1, width)
    out_re = jnp.dot(flat_re, cos_table, preferred_element_type=jnp.float32) + jnp.dot(
        flat_im, sin_table, preferred_element_type=jnp.float32
    )
    out_im = jnp.dot(flat_im, cos_table, preferred_element_type=jnp.float32) - jnp.dot(
        flat_re, sin_table, preferred_element_type=jnp.float32
    )
    return jnp.stack([out_re, out_im]).astype(jnp.bfloat16).reshape(filtered.shape)


def fb_batched(matrix, vectors):
    return jnp.einsum("ksu,kub->ksb", matrix, vectors, precision=lax.Precision.HIGHEST)


def fb_iterate(rows_re, rows_im, steer_re, steer_im, diag_total, load, collect, combine):
    weight_re = steer_re / diag_total
    weight_im = steer_im / diag_total
    for sweep_no in range(2):
        full_re, full_im = collect(weight_re, weight_im)
        prod_re = fb_batched(rows_re, full_re) - fb_batched(rows_im, full_im)
        prod_im = fb_batched(rows_re, full_im) + fb_batched(rows_im, full_re)
        prod_re, prod_im = combine(prod_re, prod_im)
        next_re = weight_re + 0.5 * (steer_re - prod_re - load * weight_re) / diag_total
        next_im = weight_im + 0.5 * (steer_im - prod_im - load * weight_im) / diag_total
        weight_re, weight_im = (next_re, next_im)
    return collect(weight_re, weight_im)


def unchanged(part_re, part_im):
    return (part_re, part_im)


def fb_local(voltages, filter_coeffs, station_gain, flags, steer_index):
    cos_table, sin_table = dft_tables(filter_coeffs.shape[1])
    row_gain = station_gain * flags[0].astype(jnp.float32)
    filtered = polyphase(voltages[:, 0], filter_coeffs, row_gain)
    local_spec = fb_transform(filtered, cos_table, sin_table)
    spectra = lax.all_to_all(local_spec, "st", split_axis=3, concat_axis=1, tiled=True)
    stations = spectra.shape[1]
    chans = spectra.shape[3]
    counted = lax.axis_size("blk") * spectra.shape[2]
    spec_re = spectra[0]
    spec_im = spectra[1]
    cov_re = jnp.einsum(
        "stk,utk->ksu", spec_re, spec_re, preferred_element_type=jnp.float32
    ) + jnp.einsum("stk,utk->ksu", spec_im, spec_im, preferred_element_type=jnp.float32)
    cov_im = jnp.einsum(
        "stk,utk->ksu", spec_im, spec_re, preferred_element_type=jnp.float32
    ) - jnp.einsum("stk,utk->ksu", spec_re, spec_im, preferred_element_type=jnp.float32)
    channel_ids = lax.axis_index("st") * chans + jnp.arange(chans, dtype=jnp.int32)
    total_re, total_im = lax.psum((cov_re, cov_im), "blk")
    rows_re = total_re / counted
    rows_im = total_im / counted
    diag_part = jnp.diagonal(rows_re, axis1=1, axis2=2)
    load = jnp.sum(diag_part, axis=1) / stations + 1e-05
    phase_int = steer_index[None, :, :] * (channel_ids + 1)[:, None, None] % PHASES
    angle = phase_int.astype(jnp.float32) * (2.0 * math.pi / PHASES)
    steer_re = jnp.cos(angle)
    steer_im = jnp.sin(angle)
    load_full = load[:, None, None]
    diag_total = (diag_part + load[:, None])[:, :, None]
    weight_re, weight_im = fb_iterate(
        rows_re, rows_im, steer_re, steer_im, diag_total, load_full, unchanged, unchanged
    )
    half_re = weight_re.astype(jnp.bfloat16)
    half_im = weight_im.astype(jnp.bfloat16)
    beam_re = jnp.einsum(
        "ksb,stk->btk", half_re, spec_re, preferred_element_type=jnp.float32
    ) + jnp.einsum("ksb,stk->btk", half_im, spec_im, preferred_element_type=jnp.float32)
    beam_im = jnp.einsum(
        "ksb,stk->btk", half_re, spec_im, preferred_element_type=jnp.float32
    ) - jnp.einsum("ksb,stk->btk", half_im, spec_re, preferred_element_type=jnp.float32)
    factor = 1.0 / math.sqrt(stations)
    beam_local = (jnp.stack([beam_re, beam_im]) * factor).astype(jnp.bfloat16)
    owned = lax.all_to_all(beam_local, "st", split_axis=1, concat_axis=3, tiled=True)
    return owned[:, :, None]


def body(voltages, filter_coeffs, station_gain, flags, steer_index):
    ndev = lax.axis_size("blk") * lax.axis_size("st")
    plan = local if filter_coeffs.shape[1] % ndev == 0 else fb_local
    return plan(voltages, filter_coeffs, station_gain, flags, steer_index)


def solution(mesh):
    return jax.shard_map(
        body,
        mesh=mesh,
        in_specs=(P(None, "blk", "st", None), P(), P("st"), P("blk", "st"), P()),
        out_specs=P(None, "st", "blk", None, None),
        check_vma=False,
    )
```

```python
import math

import jax
import jax.numpy as jnp
from jax import lax
from jax.sharding import PartitionSpec as P

PHASES = 4096
AXES = ("blk", "st")


def dft_tables(width):
    counter = jnp.arange(width, dtype=jnp.int32)
    product = counter[:, None] * counter[None, :] % width
    angle = product.astype(jnp.float32) * (2.0 * math.pi / width)
    factor = 1.0 / math.sqrt(width)
    return (
        (jnp.cos(angle) * factor).astype(jnp.bfloat16),
        (jnp.sin(angle) * factor).astype(jnp.bfloat16),
    )


def polyphase(samples, filter_coeffs, row_gain):
    ntaps = filter_coeffs.shape[0]
    width = filter_coeffs.shape[1]
    grid = samples.astype(jnp.float32).reshape(2, samples.shape[1], -1, width)
    count = grid.shape[2] - ntaps + 1
    filtered = filter_coeffs[0][None, None, None, :] * grid[:, :, 0:count, :]
    for tap_no in range(1, ntaps):
        filtered = (
            filtered
            + filter_coeffs[tap_no][None, None, None, :] * grid[:, :, tap_no : tap_no + count, :]
        )
    return (filtered * row_gain[None, :, None, None]).astype(jnp.bfloat16)


def polyphase_flat(samples, filter_coeffs, row_gain):
    ntaps = filter_coeffs.shape[0]
    width = filter_coeffs.shape[1]
    count = samples.shape[2] // width - ntaps + 1
    span = count * width
    coeffs = jnp.tile(filter_coeffs, (1, count))
    filtered = coeffs[0][None, None, :] * samples[:, :, 0:span].astype(jnp.float32)
    for tap_no in range(1, ntaps):
        window = samples[:, :, tap_no * width : tap_no * width + span].astype(jnp.float32)
        filtered = filtered + coeffs[tap_no][None, None, :] * window
    filtered = (filtered * row_gain[None, :, None]).astype(jnp.bfloat16)
    return filtered.reshape(samples.shape[0], samples.shape[1], count, width)


def transform(filtered, cos_table, sin_table):
    flat_re = filtered[0]
    flat_im = filtered[1]
    dot = lambda a, b: jnp.einsum("stc,ck->stk", a, b, preferred_element_type=jnp.float32)
    out_re = dot(flat_re, cos_table) + dot(flat_im, sin_table)
    out_im = dot(flat_im, cos_table) - dot(flat_re, sin_table)
    return jnp.stack([out_re, out_im]).astype(jnp.bfloat16)


def batched(matrix, vectors):
    return jnp.einsum("ksu,kub->ksb", matrix, vectors, precision=lax.Precision.HIGHEST)


def iterate(rows_re, rows_im, steer_re, steer_im, diag_total, load):
    weight_re = steer_re / diag_total
    weight_im = steer_im / diag_total
    for sweep_no in range(2):
        prod_re = batched(rows_re, weight_re) - batched(rows_im, weight_im)
        prod_im = batched(rows_re, weight_im) + batched(rows_im, weight_re)
        next_re = weight_re + 0.5 * (steer_re - prod_re - load * weight_re) / diag_total
        next_im = weight_im + 0.5 * (steer_im - prod_im - load * weight_im) / diag_total
        weight_re, weight_im = (next_re, next_im)
    return weight_re, weight_im


def local(voltages, filter_coeffs, station_gain, flags, steer_index):
    nblk = lax.axis_size("blk")
    nst = lax.axis_size("st")
    ndev = nblk * nst
    ntaps, nk = filter_coeffs.shape
    cos_table, sin_table = dft_tables(nk)
    row_gain = station_gain * flags[0].astype(jnp.float32)
    samples = voltages[:, 0]
    ls = samples.shape[1]
    nt = samples.shape[2] // nk - ntaps + 1
    kc = nk // ndev
    stations = nst * ls
    counted = nblk * nt
    ngr = 4 if ls % 64 == 0 else 1
    gs = ls // ngr
    me = lax.axis_index("blk") * nst + lax.axis_index("st")
    eye = jnp.eye(stations, dtype=jnp.float32)
    factor = 1.0 / math.sqrt(stations)
    arrived = []
    for g in range(ngr):
        part = samples[:, g * gs : (g + 1) * gs]
        filtered = polyphase_flat(part, filter_coeffs, row_gain[g * gs : (g + 1) * gs])
        local_spec = transform(filtered, cos_table, sin_table)
        send = local_spec.reshape(2, gs, nt, ndev, kc).transpose(3, 4, 0, 1, 2)
        if g < ngr - 1:
            arrived.append(lax.all_to_all(send, AXES, split_axis=0, concat_axis=0, tiled=True))
        else:
            last = [
                lax.all_to_all(send[:, c], AXES, split_axis=0, concat_axis=0, tiled=True)
                for c in range(kc)
            ]
    hi = lax.Precision.HIGHEST
    got = []
    prev = None
    for c in range(kc):
        pieces = [part[:, c] for part in arrived] + [last[c]]
        if prev is not None:
            pieces, _ = lax.optimization_barrier((pieces, prev))
        recv = jnp.stack(pieces, axis=2).reshape(nblk, nst, 2, ngr, gs, nt)
        spec = recv.transpose(2, 1, 3, 4, 0, 5).reshape(2 * stations, counted)
        gram = jnp.dot(spec, spec.T, preferred_element_type=jnp.float32)
        g00 = gram[:stations, :stations]
        g01 = gram[:stations, stations:]
        g10 = gram[stations:, :stations]
        g11 = gram[stations:, stations:]
        rows_re = (g00 + g11) / counted
        rows_im = (g10 - g01) / counted
        rows = jnp.concatenate([rows_re, rows_im], axis=0)
        diag_part = jnp.sum(rows_re * eye, axis=1)
        load = jnp.sum(diag_part) / stations + 1e-05
        channel_no = me * kc + c
        phase_int = steer_index * (channel_no + 1) % PHASES
        angle = phase_int.astype(jnp.float32) * (2.0 * math.pi / PHASES)
        steer_re = jnp.cos(angle)
        steer_im = jnp.sin(angle)
        diag_total = (diag_part + load)[:, None]
        weight_re = steer_re / diag_total
        weight_im = steer_im / diag_total
        nb = weight_re.shape[1]
        for sweep_no in range(2):
            both = jnp.concatenate([weight_re, weight_im], axis=1)
            prod = jnp.dot(rows, both, precision=hi)
            prod_re = prod[:stations, :nb] - prod[stations:, nb:]
            prod_im = prod[:stations, nb:] + prod[stations:, :nb]
            next_re = weight_re + 0.5 * (steer_re - prod_re - load * weight_re) / diag_total
            next_im = weight_im + 0.5 * (steer_im - prod_im - load * weight_im) / diag_total
            weight_re, weight_im = (next_re, next_im)
        half_re = weight_re.astype(jnp.bfloat16)
        half_im = weight_im.astype(jnp.bfloat16)
        lhs = jnp.concatenate(
            [jnp.concatenate([half_re, -half_im], axis=1), jnp.concatenate([half_im, half_re], axis=1)],
            axis=0,
        )
        beam = jnp.dot(lhs.T, spec, preferred_element_type=jnp.float32)
        beam = (beam * factor).astype(jnp.bfloat16)
        bc = nb // nst
        out = beam.reshape(2, nst, bc, nblk, nt).transpose(3, 1, 0, 2, 4).reshape(ndev, 2, bc, nt)
        prev = out
        got.append(lax.all_to_all(out, AXES, split_axis=0, concat_axis=0, tiled=True))
    res = jnp.stack(got, axis=4).transpose(1, 2, 3, 0, 4).reshape(2, bc, nt, ndev * kc)
    return res[:, :, None]


def fb_transform(filtered, cos_table, sin_table):
    width = cos_table.shape[0]
    flat_re = filtered[0].reshape(-1, width)
    flat_im = filtered[1].reshape(-1, width)
    out_re = jnp.dot(flat_re, cos_table, preferred_element_type=jnp.float32) + jnp.dot(
        flat_im, sin_table, preferred_element_type=jnp.float32
    )
    out_im = jnp.dot(flat_im, cos_table, preferred_element_type=jnp.float32) - jnp.dot(
        flat_re, sin_table, preferred_element_type=jnp.float32
    )
    return jnp.stack([out_re, out_im]).astype(jnp.bfloat16).reshape(filtered.shape)


def fb_batched(matrix, vectors):
    return jnp.einsum("ksu,kub->ksb", matrix, vectors, precision=lax.Precision.HIGHEST)


def fb_iterate(rows_re, rows_im, steer_re, steer_im, diag_total, load, collect, combine):
    weight_re = steer_re / diag_total
    weight_im = steer_im / diag_total
    for sweep_no in range(2):
        full_re, full_im = collect(weight_re, weight_im)
        prod_re = fb_batched(rows_re, full_re) - fb_batched(rows_im, full_im)
        prod_im = fb_batched(rows_re, full_im) + fb_batched(rows_im, full_re)
        prod_re, prod_im = combine(prod_re, prod_im)
        next_re = weight_re + 0.5 * (steer_re - prod_re - load * weight_re) / diag_total
        next_im = weight_im + 0.5 * (steer_im - prod_im - load * weight_im) / diag_total
        weight_re, weight_im = (next_re, next_im)
    return collect(weight_re, weight_im)


def unchanged(part_re, part_im):
    return (part_re, part_im)


def fb_local(voltages, filter_coeffs, station_gain, flags, steer_index):
    cos_table, sin_table = dft_tables(filter_coeffs.shape[1])
    row_gain = station_gain * flags[0].astype(jnp.float32)
    filtered = polyphase(voltages[:, 0], filter_coeffs, row_gain)
    local_spec = fb_transform(filtered, cos_table, sin_table)
    spectra = lax.all_to_all(local_spec, "st", split_axis=3, concat_axis=1, tiled=True)
    stations = spectra.shape[1]
    chans = spectra.shape[3]
    counted = lax.axis_size("blk") * spectra.shape[2]
    spec_re = spectra[0]
    spec_im = spectra[1]
    cov_re = jnp.einsum(
        "stk,utk->ksu", spec_re, spec_re, preferred_element_type=jnp.float32
    ) + jnp.einsum("stk,utk->ksu", spec_im, spec_im, preferred_element_type=jnp.float32)
    cov_im = jnp.einsum(
        "stk,utk->ksu", spec_im, spec_re, preferred_element_type=jnp.float32
    ) - jnp.einsum("stk,utk->ksu", spec_re, spec_im, preferred_element_type=jnp.float32)
    channel_ids = lax.axis_index("st") * chans + jnp.arange(chans, dtype=jnp.int32)
    total_re, total_im = lax.psum((cov_re, cov_im), "blk")
    rows_re = total_re / counted
    rows_im = total_im / counted
    diag_part = jnp.diagonal(rows_re, axis1=1, axis2=2)
    load = jnp.sum(diag_part, axis=1) / stations + 1e-05
    phase_int = steer_index[None, :, :] * (channel_ids + 1)[:, None, None] % PHASES
    angle = phase_int.astype(jnp.float32) * (2.0 * math.pi / PHASES)
    steer_re = jnp.cos(angle)
    steer_im = jnp.sin(angle)
    load_full = load[:, None, None]
    diag_total = (diag_part + load[:, None])[:, :, None]
    weight_re, weight_im = fb_iterate(
        rows_re, rows_im, steer_re, steer_im, diag_total, load_full, unchanged, unchanged
    )
    half_re = weight_re.astype(jnp.bfloat16)
    half_im = weight_im.astype(jnp.bfloat16)
    beam_re = jnp.einsum(
        "ksb,stk->btk", half_re, spec_re, preferred_element_type=jnp.float32
    ) + jnp.einsum("ksb,stk->btk", half_im, spec_im, preferred_element_type=jnp.float32)
    beam_im = jnp.einsum(
        "ksb,stk->btk", half_re, spec_im, preferred_element_type=jnp.float32
    ) - jnp.einsum("ksb,stk->btk", half_im, spec_re, preferred_element_type=jnp.float32)
    factor = 1.0 / math.sqrt(stations)
    beam_local = (jnp.stack([beam_re, beam_im]) * factor).astype(jnp.bfloat16)
    owned = lax.all_to_all(beam_local, "st", split_axis=1, concat_axis=3, tiled=True)
    return owned[:, :, None]


def body(voltages, filter_coeffs, station_gain, flags, steer_index):
    ndev = lax.axis_size("blk") * lax.axis_size("st")
    plan = local if filter_coeffs.shape[1] % ndev == 0 else fb_local
    return plan(voltages, filter_coeffs, station_gain, flags, steer_index)


def solution(mesh):
    return jax.shard_map(
        body,
        mesh=mesh,
        in_specs=(P(None, "blk", "st", None), P(), P("st"), P("blk", "st"), P()),
        out_specs=P(None, "st", "blk", None, None),
        check_vma=False,
    )
```

```python
import math

import jax
import jax.numpy as jnp
from jax import lax
from jax.sharding import PartitionSpec as P

PHASES = 4096
AXES = ("blk", "st")


def dft_tables(width):
    counter = jnp.arange(width, dtype=jnp.int32)
    product = counter[:, None] * counter[None, :] % width
    angle = product.astype(jnp.float32) * (2.0 * math.pi / width)
    factor = 1.0 / math.sqrt(width)
    return (
        (jnp.cos(angle) * factor).astype(jnp.bfloat16),
        (jnp.sin(angle) * factor).astype(jnp.bfloat16),
    )


def polyphase(samples, filter_coeffs, row_gain):
    ntaps = filter_coeffs.shape[0]
    width = filter_coeffs.shape[1]
    grid = samples.astype(jnp.float32).reshape(2, samples.shape[1], -1, width)
    count = grid.shape[2] - ntaps + 1
    filtered = filter_coeffs[0][None, None, None, :] * grid[:, :, 0:count, :]
    for tap_no in range(1, ntaps):
        filtered = (
            filtered
            + filter_coeffs[tap_no][None, None, None, :] * grid[:, :, tap_no : tap_no + count, :]
        )
    return (filtered * row_gain[None, :, None, None]).astype(jnp.bfloat16)


def polyphase_flat(samples, filter_coeffs, row_gain):
    ntaps = filter_coeffs.shape[0]
    width = filter_coeffs.shape[1]
    count = samples.shape[2] // width - ntaps + 1
    span = count * width
    coeffs = jnp.tile(filter_coeffs, (1, count))
    filtered = coeffs[0][None, None, :] * samples[:, :, 0:span].astype(jnp.float32)
    for tap_no in range(1, ntaps):
        window = samples[:, :, tap_no * width : tap_no * width + span].astype(jnp.float32)
        filtered = filtered + coeffs[tap_no][None, None, :] * window
    filtered = (filtered * row_gain[None, :, None]).astype(jnp.bfloat16)
    return filtered.reshape(samples.shape[0], samples.shape[1], count, width)


def transform(filtered, cos_table, sin_table):
    flat_re = filtered[0]
    flat_im = filtered[1]
    dot = lambda a, b: jnp.einsum("stc,ck->stk", a, b, preferred_element_type=jnp.float32)
    out_re = dot(flat_re, cos_table) + dot(flat_im, sin_table)
    out_im = dot(flat_im, cos_table) - dot(flat_re, sin_table)
    return jnp.stack([out_re, out_im]).astype(jnp.bfloat16)


def batched(matrix, vectors):
    return jnp.einsum("ksu,kub->ksb", matrix, vectors, precision=lax.Precision.HIGHEST)


def iterate(rows_re, rows_im, steer_re, steer_im, diag_total, load):
    weight_re = steer_re / diag_total
    weight_im = steer_im / diag_total
    for sweep_no in range(2):
        prod_re = batched(rows_re, weight_re) - batched(rows_im, weight_im)
        prod_im = batched(rows_re, weight_im) + batched(rows_im, weight_re)
        next_re = weight_re + 0.5 * (steer_re - prod_re - load * weight_re) / diag_total
        next_im = weight_im + 0.5 * (steer_im - prod_im - load * weight_im) / diag_total
        weight_re, weight_im = (next_re, next_im)
    return weight_re, weight_im


def local(voltages, filter_coeffs, station_gain, flags, steer_index):
    nblk = lax.axis_size("blk")
    nst = lax.axis_size("st")
    ndev = nblk * nst
    ntaps, nk = filter_coeffs.shape
    cos_table, sin_table = dft_tables(nk)
    row_gain = station_gain * flags[0].astype(jnp.float32)
    samples = voltages[:, 0]
    ls = samples.shape[1]
    nt = samples.shape[2] // nk - ntaps + 1
    kc = nk // ndev
    stations = nst * ls
    counted = nblk * nt
    ngr = 4 if ls % 64 == 0 else 1
    gs = ls // ngr
    me = lax.axis_index("blk") * nst + lax.axis_index("st")
    eye = jnp.eye(stations, dtype=jnp.float32)
    factor = 1.0 / math.sqrt(stations)
    arrived = []
    later = []
    for g in range(ngr):
        part = samples[:, g * gs : (g + 1) * gs]
        filtered = polyphase_flat(part, filter_coeffs, row_gain[g * gs : (g + 1) * gs])
        local_spec = transform(filtered, cos_table, sin_table)
        send = local_spec.reshape(2, gs, nt, ndev, kc).transpose(3, 4, 0, 1, 2)
        if g == 0:
            arrived.append(lax.all_to_all(send, AXES, split_axis=0, concat_axis=0, tiled=True))
        else:
            later.append(send)
    last = [
        lax.all_to_all(
            jnp.stack([part[:, c] for part in later], axis=1), AXES, split_axis=0, concat_axis=0, tiled=True
        )
        for c in range(kc)
        if later
    ]
    hi = lax.Precision.HIGHEST
    got = []
    prev = None
    for c in range(kc):
        pieces = [part[:, c] for part in arrived] + [last[c][:, i] for i in range(len(later))]
        if prev is not None:
            pieces, _ = lax.optimization_barrier((pieces, prev))
        recv = jnp.stack(pieces, axis=2).reshape(nblk, nst, 2, ngr, gs, nt)
        spec = recv.transpose(2, 1, 3, 4, 0, 5).reshape(2 * stations, counted)
        gram = jnp.dot(spec, spec.T, preferred_element_type=jnp.float32)
        g00 = gram[:stations, :stations]
        g01 = gram[:stations, stations:]
        g10 = gram[stations:, :stations]
        g11 = gram[stations:, stations:]
        rows_re = (g00 + g11) / counted
        rows_im = (g10 - g01) / counted
        rows = jnp.concatenate([rows_re, rows_im], axis=0)
        diag_part = jnp.sum(rows_re * eye, axis=1)
        load = jnp.sum(diag_part) / stations + 1e-05
        channel_no = me * kc + c
        phase_int = steer_index * (channel_no + 1) % PHASES
        angle = phase_int.astype(jnp.float32) * (2.0 * math.pi / PHASES)
        steer_re = jnp.cos(angle)
        steer_im = jnp.sin(angle)
        diag_total = (diag_part + load)[:, None]
        weight_re = steer_re / diag_total
        weight_im = steer_im / diag_total
        nb = weight_re.shape[1]
        for sweep_no in range(2):
            both = jnp.concatenate([weight_re, weight_im], axis=1)
            prod = jnp.dot(rows, both, precision=hi)
            prod_re = prod[:stations, :nb] - prod[stations:, nb:]
            prod_im = prod[:stations, nb:] + prod[stations:, :nb]
            next_re = weight_re + 0.5 * (steer_re - prod_re - load * weight_re) / diag_total
            next_im = weight_im + 0.5 * (steer_im - prod_im - load * weight_im) / diag_total
            weight_re, weight_im = (next_re, next_im)
        half_re = weight_re.astype(jnp.bfloat16)
        half_im = weight_im.astype(jnp.bfloat16)
        lhs = jnp.concatenate(
            [jnp.concatenate([half_re, -half_im], axis=1), jnp.concatenate([half_im, half_re], axis=1)],
            axis=0,
        )
        beam = jnp.dot(lhs.T, spec, preferred_element_type=jnp.float32)
        beam = (beam * factor).astype(jnp.bfloat16)
        bc = nb // nst
        out = beam.reshape(2, nst, bc, nblk, nt).transpose(3, 1, 0, 2, 4).reshape(ndev, 2, bc, nt)
        prev = out
        got.append(lax.all_to_all(out, AXES, split_axis=0, concat_axis=0, tiled=True))
    res = jnp.stack(got, axis=4).transpose(1, 2, 3, 0, 4).reshape(2, bc, nt, ndev * kc)
    return res[:, :, None]


def fb_transform(filtered, cos_table, sin_table):
    width = cos_table.shape[0]
    flat_re = filtered[0].reshape(-1, width)
    flat_im = filtered[1].reshape(-1, width)
    out_re = jnp.dot(flat_re, cos_table, preferred_element_type=jnp.float32) + jnp.dot(
        flat_im, sin_table, preferred_element_type=jnp.float32
    )
    out_im = jnp.dot(flat_im, cos_table, preferred_element_type=jnp.float32) - jnp.dot(
        flat_re, sin_table, preferred_element_type=jnp.float32
    )
    return jnp.stack([out_re, out_im]).astype(jnp.bfloat16).reshape(filtered.shape)


def fb_batched(matrix, vectors):
    return jnp.einsum("ksu,kub->ksb", matrix, vectors, precision=lax.Precision.HIGHEST)


def fb_iterate(rows_re, rows_im, steer_re, steer_im, diag_total, load, collect, combine):
    weight_re = steer_re / diag_total
    weight_im = steer_im / diag_total
    for sweep_no in range(2):
        full_re, full_im = collect(weight_re, weight_im)
        prod_re = fb_batched(rows_re, full_re) - fb_batched(rows_im, full_im)
        prod_im = fb_batched(rows_re, full_im) + fb_batched(rows_im, full_re)
        prod_re, prod_im = combine(prod_re, prod_im)
        next_re = weight_re + 0.5 * (steer_re - prod_re - load * weight_re) / diag_total
        next_im = weight_im + 0.5 * (steer_im - prod_im - load * weight_im) / diag_total
        weight_re, weight_im = (next_re, next_im)
    return collect(weight_re, weight_im)


def unchanged(part_re, part_im):
    return (part_re, part_im)


def fb_local(voltages, filter_coeffs, station_gain, flags, steer_index):
    cos_table, sin_table = dft_tables(filter_coeffs.shape[1])
    row_gain = station_gain * flags[0].astype(jnp.float32)
    filtered = polyphase(voltages[:, 0], filter_coeffs, row_gain)
    local_spec = fb_transform(filtered, cos_table, sin_table)
    spectra = lax.all_to_all(local_spec, "st", split_axis=3, concat_axis=1, tiled=True)
    stations = spectra.shape[1]
    chans = spectra.shape[3]
    counted = lax.axis_size("blk") * spectra.shape[2]
    spec_re = spectra[0]
    spec_im = spectra[1]
    cov_re = jnp.einsum(
        "stk,utk->ksu", spec_re, spec_re, preferred_element_type=jnp.float32
    ) + jnp.einsum("stk,utk->ksu", spec_im, spec_im, preferred_element_type=jnp.float32)
    cov_im = jnp.einsum(
        "stk,utk->ksu", spec_im, spec_re, preferred_element_type=jnp.float32
    ) - jnp.einsum("stk,utk->ksu", spec_re, spec_im, preferred_element_type=jnp.float32)
    channel_ids = lax.axis_index("st") * chans + jnp.arange(chans, dtype=jnp.int32)
    total_re, total_im = lax.psum((cov_re, cov_im), "blk")
    rows_re = total_re / counted
    rows_im = total_im / counted
    diag_part = jnp.diagonal(rows_re, axis1=1, axis2=2)
    load = jnp.sum(diag_part, axis=1) / stations + 1e-05
    phase_int = steer_index[None, :, :] * (channel_ids + 1)[:, None, None] % PHASES
    angle = phase_int.astype(jnp.float32) * (2.0 * math.pi / PHASES)
    steer_re = jnp.cos(angle)
    steer_im = jnp.sin(angle)
    load_full = load[:, None, None]
    diag_total = (diag_part + load[:, None])[:, :, None]
    weight_re, weight_im = fb_iterate(
        rows_re, rows_im, steer_re, steer_im, diag_total, load_full, unchanged, unchanged
    )
    half_re = weight_re.astype(jnp.bfloat16)
    half_im = weight_im.astype(jnp.bfloat16)
    beam_re = jnp.einsum(
        "ksb,stk->btk", half_re, spec_re, preferred_element_type=jnp.float32
    ) + jnp.einsum("ksb,stk->btk", half_im, spec_im, preferred_element_type=jnp.float32)
    beam_im = jnp.einsum(
        "ksb,stk->btk", half_re, spec_im, preferred_element_type=jnp.float32
    ) - jnp.einsum("ksb,stk->btk", half_im, spec_re, preferred_element_type=jnp.float32)
    factor = 1.0 / math.sqrt(stations)
    beam_local = (jnp.stack([beam_re, beam_im]) * factor).astype(jnp.bfloat16)
    owned = lax.all_to_all(beam_local, "st", split_axis=1, concat_axis=3, tiled=True)
    return owned[:, :, None]


def body(voltages, filter_coeffs, station_gain, flags, steer_index):
    ndev = lax.axis_size("blk") * lax.axis_size("st")
    plan = local if filter_coeffs.shape[1] % ndev == 0 else fb_local
    return plan(voltages, filter_coeffs, station_gain, flags, steer_index)


def solution(mesh):
    return jax.shard_map(
        body,
        mesh=mesh,
        in_specs=(P(None, "blk", "st", None), P(), P("st"), P("blk", "st"), P()),
        out_specs=P(None, "st", "blk", None, None),
        check_vma=False,
    )
```

```python
import math

import jax
import jax.numpy as jnp
from jax import lax
from jax.sharding import PartitionSpec as P

PHASES = 4096
AXES = ("blk", "st")


def dft_tables(width):
    counter = jnp.arange(width, dtype=jnp.int32)
    product = counter[:, None] * counter[None, :] % width
    angle = product.astype(jnp.float32) * (2.0 * math.pi / width)
    factor = 1.0 / math.sqrt(width)
    return (
        (jnp.cos(angle) * factor).astype(jnp.bfloat16),
        (jnp.sin(angle) * factor).astype(jnp.bfloat16),
    )


def polyphase(samples, filter_coeffs, row_gain):
    ntaps = filter_coeffs.shape[0]
    width = filter_coeffs.shape[1]
    grid = samples.astype(jnp.float32).reshape(2, samples.shape[1], -1, width)
    count = grid.shape[2] - ntaps + 1
    filtered = filter_coeffs[0][None, None, None, :] * grid[:, :, 0:count, :]
    for tap_no in range(1, ntaps):
        filtered = (
            filtered
            + filter_coeffs[tap_no][None, None, None, :] * grid[:, :, tap_no : tap_no + count, :]
        )
    return (filtered * row_gain[None, :, None, None]).astype(jnp.bfloat16)


def polyphase_flat(samples, filter_coeffs, row_gain):
    ntaps = filter_coeffs.shape[0]
    width = filter_coeffs.shape[1]
    count = samples.shape[2] // width - ntaps + 1
    span = count * width
    coeffs = jnp.tile(filter_coeffs, (1, count))
    filtered = coeffs[0][None, None, :] * samples[:, :, 0:span].astype(jnp.float32)
    for tap_no in range(1, ntaps):
        window = samples[:, :, tap_no * width : tap_no * width + span].astype(jnp.float32)
        filtered = filtered + coeffs[tap_no][None, None, :] * window
    filtered = (filtered * row_gain[None, :, None]).astype(jnp.bfloat16)
    return filtered.reshape(samples.shape[0], samples.shape[1], count, width)


def transform(filtered, cos_table, sin_table):
    flat_re = filtered[0]
    flat_im = filtered[1]
    dot = lambda a, b: jnp.einsum("stc,ck->stk", a, b, preferred_element_type=jnp.float32)
    out_re = dot(flat_re, cos_table) + dot(flat_im, sin_table)
    out_im = dot(flat_im, cos_table) - dot(flat_re, sin_table)
    return jnp.stack([out_re, out_im]).astype(jnp.bfloat16)


def batched(matrix, vectors):
    return jnp.einsum("ksu,kub->ksb", matrix, vectors, precision=lax.Precision.HIGHEST)


def iterate(rows_re, rows_im, steer_re, steer_im, diag_total, load):
    weight_re = steer_re / diag_total
    weight_im = steer_im / diag_total
    for sweep_no in range(2):
        prod_re = batched(rows_re, weight_re) - batched(rows_im, weight_im)
        prod_im = batched(rows_re, weight_im) + batched(rows_im, weight_re)
        next_re = weight_re + 0.5 * (steer_re - prod_re - load * weight_re) / diag_total
        next_im = weight_im + 0.5 * (steer_im - prod_im - load * weight_im) / diag_total
        weight_re, weight_im = (next_re, next_im)
    return weight_re, weight_im


def local(voltages, filter_coeffs, station_gain, flags, steer_index):
    nblk = lax.axis_size("blk")
    nst = lax.axis_size("st")
    ndev = nblk * nst
    ntaps, nk = filter_coeffs.shape
    cos_table, sin_table = dft_tables(nk)
    row_gain = station_gain * flags[0].astype(jnp.float32)
    samples = voltages[:, 0]
    ls = samples.shape[1]
    nt = samples.shape[2] // nk - ntaps + 1
    kc = nk // ndev
    stations = nst * ls
    counted = nblk * nt
    ngr = 4 if ls % 64 == 0 else 1
    gs = ls // ngr
    me = lax.axis_index("blk") * nst + lax.axis_index("st")
    eye = jnp.eye(stations, dtype=jnp.float32)
    factor = 1.0 / math.sqrt(stations)
    arrived = []
    later = []
    for g in range(ngr):
        part = samples[:, g * gs : (g + 1) * gs]
        filtered = polyphase_flat(part, filter_coeffs, row_gain[g * gs : (g + 1) * gs])
        local_spec = transform(filtered, cos_table, sin_table)
        send = local_spec.reshape(2, gs, nt, ndev, kc).transpose(3, 4, 0, 1, 2)
        if g == 0:
            arrived.append(lax.all_to_all(send, AXES, split_axis=0, concat_axis=0, tiled=True))
        else:
            later.append(send)
    if later:
        later, arrived = lax.optimization_barrier((later, arrived))
    last = [
        lax.all_to_all(
            jnp.stack([part[:, c] for part in later], axis=1), AXES, split_axis=0, concat_axis=0, tiled=True
        )
        for c in range(kc)
        if later
    ]
    hi = lax.Precision.HIGHEST
    got = []
    prev = None
    for c in range(kc):
        pieces = [part[:, c] for part in arrived] + [last[c][:, i] for i in range(len(later))]
        if prev is not None:
            pieces, _ = lax.optimization_barrier((pieces, prev))
        recv = jnp.stack(pieces, axis=2).reshape(nblk, nst, 2, ngr, gs, nt)
        spec = recv.transpose(2, 1, 3, 4, 0, 5).reshape(2 * stations, counted)
        gram = jnp.dot(spec, spec.T, preferred_element_type=jnp.float32)
        g00 = gram[:stations, :stations]
        g01 = gram[:stations, stations:]
        g10 = gram[stations:, :stations]
        g11 = gram[stations:, stations:]
        rows_re = (g00 + g11) / counted
        rows_im = (g10 - g01) / counted
        rows = jnp.concatenate([rows_re, rows_im], axis=0)
        diag_part = jnp.sum(rows_re * eye, axis=1)
        load = jnp.sum(diag_part) / stations + 1e-05
        channel_no = me * kc + c
        phase_int = steer_index * (channel_no + 1) % PHASES
        angle = phase_int.astype(jnp.float32) * (2.0 * math.pi / PHASES)
        steer_re = jnp.cos(angle)
        steer_im = jnp.sin(angle)
        diag_total = (diag_part + load)[:, None]
        weight_re = steer_re / diag_total
        weight_im = steer_im / diag_total
        nb = weight_re.shape[1]
        for sweep_no in range(2):
            both = jnp.concatenate([weight_re, weight_im], axis=1)
            prod = jnp.dot(rows, both, precision=hi)
            prod_re = prod[:stations, :nb] - prod[stations:, nb:]
            prod_im = prod[:stations, nb:] + prod[stations:, :nb]
            next_re = weight_re + 0.5 * (steer_re - prod_re - load * weight_re) / diag_total
            next_im = weight_im + 0.5 * (steer_im - prod_im - load * weight_im) / diag_total
            weight_re, weight_im = (next_re, next_im)
        half_re = weight_re.astype(jnp.bfloat16)
        half_im = weight_im.astype(jnp.bfloat16)
        lhs = jnp.concatenate(
            [jnp.concatenate([half_re, -half_im], axis=1), jnp.concatenate([half_im, half_re], axis=1)],
            axis=0,
        )
        beam = jnp.dot(lhs.T, spec, preferred_element_type=jnp.float32)
        beam = (beam * factor).astype(jnp.bfloat16)
        bc = nb // nst
        out = beam.reshape(2, nst, bc, nblk, nt).transpose(3, 1, 0, 2, 4).reshape(ndev, 2, bc, nt)
        prev = out
        got.append(lax.all_to_all(out, AXES, split_axis=0, concat_axis=0, tiled=True))
    res = jnp.stack(got, axis=4).transpose(1, 2, 3, 0, 4).reshape(2, bc, nt, ndev * kc)
    return res[:, :, None]


def fb_transform(filtered, cos_table, sin_table):
    width = cos_table.shape[0]
    flat_re = filtered[0].reshape(-1, width)
    flat_im = filtered[1].reshape(-1, width)
    out_re = jnp.dot(flat_re, cos_table, preferred_element_type=jnp.float32) + jnp.dot(
        flat_im, sin_table, preferred_element_type=jnp.float32
    )
    out_im = jnp.dot(flat_im, cos_table, preferred_element_type=jnp.float32) - jnp.dot(
        flat_re, sin_table, preferred_element_type=jnp.float32
    )
    return jnp.stack([out_re, out_im]).astype(jnp.bfloat16).reshape(filtered.shape)


def fb_batched(matrix, vectors):
    return jnp.einsum("ksu,kub->ksb", matrix, vectors, precision=lax.Precision.HIGHEST)


def fb_iterate(rows_re, rows_im, steer_re, steer_im, diag_total, load, collect, combine):
    weight_re = steer_re / diag_total
    weight_im = steer_im / diag_total
    for sweep_no in range(2):
        full_re, full_im = collect(weight_re, weight_im)
        prod_re = fb_batched(rows_re, full_re) - fb_batched(rows_im, full_im)
        prod_im = fb_batched(rows_re, full_im) + fb_batched(rows_im, full_re)
        prod_re, prod_im = combine(prod_re, prod_im)
        next_re = weight_re + 0.5 * (steer_re - prod_re - load * weight_re) / diag_total
        next_im = weight_im + 0.5 * (steer_im - prod_im - load * weight_im) / diag_total
        weight_re, weight_im = (next_re, next_im)
    return collect(weight_re, weight_im)


def unchanged(part_re, part_im):
    return (part_re, part_im)


def fb_local(voltages, filter_coeffs, station_gain, flags, steer_index):
    cos_table, sin_table = dft_tables(filter_coeffs.shape[1])
    row_gain = station_gain * flags[0].astype(jnp.float32)
    filtered = polyphase(voltages[:, 0], filter_coeffs, row_gain)
    local_spec = fb_transform(filtered, cos_table, sin_table)
    spectra = lax.all_to_all(local_spec, "st", split_axis=3, concat_axis=1, tiled=True)
    stations = spectra.shape[1]
    chans = spectra.shape[3]
    counted = lax.axis_size("blk") * spectra.shape[2]
    spec_re = spectra[0]
    spec_im = spectra[1]
    cov_re = jnp.einsum(
        "stk,utk->ksu", spec_re, spec_re, preferred_element_type=jnp.float32
    ) + jnp.einsum("stk,utk->ksu", spec_im, spec_im, preferred_element_type=jnp.float32)
    cov_im = jnp.einsum(
        "stk,utk->ksu", spec_im, spec_re, preferred_element_type=jnp.float32
    ) - jnp.einsum("stk,utk->ksu", spec_re, spec_im, preferred_element_type=jnp.float32)
    channel_ids = lax.axis_index("st") * chans + jnp.arange(chans, dtype=jnp.int32)
    total_re, total_im = lax.psum((cov_re, cov_im), "blk")
    rows_re = total_re / counted
    rows_im = total_im / counted
    diag_part = jnp.diagonal(rows_re, axis1=1, axis2=2)
    load = jnp.sum(diag_part, axis=1) / stations + 1e-05
    phase_int = steer_index[None, :, :] * (channel_ids + 1)[:, None, None] % PHASES
    angle = phase_int.astype(jnp.float32) * (2.0 * math.pi / PHASES)
    steer_re = jnp.cos(angle)
    steer_im = jnp.sin(angle)
    load_full = load[:, None, None]
    diag_total = (diag_part + load[:, None])[:, :, None]
    weight_re, weight_im = fb_iterate(
        rows_re, rows_im, steer_re, steer_im, diag_total, load_full, unchanged, unchanged
    )
    half_re = weight_re.astype(jnp.bfloat16)
    half_im = weight_im.astype(jnp.bfloat16)
    beam_re = jnp.einsum(
        "ksb,stk->btk", half_re, spec_re, preferred_element_type=jnp.float32
    ) + jnp.einsum("ksb,stk->btk", half_im, spec_im, preferred_element_type=jnp.float32)
    beam_im = jnp.einsum(
        "ksb,stk->btk", half_re, spec_im, preferred_element_type=jnp.float32
    ) - jnp.einsum("ksb,stk->btk", half_im, spec_re, preferred_element_type=jnp.float32)
    factor = 1.0 / math.sqrt(stations)
    beam_local = (jnp.stack([beam_re, beam_im]) * factor).astype(jnp.bfloat16)
    owned = lax.all_to_all(beam_local, "st", split_axis=1, concat_axis=3, tiled=True)
    return owned[:, :, None]


def body(voltages, filter_coeffs, station_gain, flags, steer_index):
    ndev = lax.axis_size("blk") * lax.axis_size("st")
    plan = local if filter_coeffs.shape[1] % ndev == 0 else fb_local
    return plan(voltages, filter_coeffs, station_gain, flags, steer_index)


def solution(mesh):
    return jax.shard_map(
        body,
        mesh=mesh,
        in_specs=(P(None, "blk", "st", None), P(), P("st"), P("blk", "st"), P()),
        out_specs=P(None, "st", "blk", None, None),
        check_vma=False,
    )
```

```python
import math

import jax
import jax.numpy as jnp
from jax import lax
from jax.sharding import PartitionSpec as P

PHASES = 4096
AXES = ("blk", "st")


def dft_tables(width):
    counter = jnp.arange(width, dtype=jnp.int32)
    product = counter[:, None] * counter[None, :] % width
    angle = product.astype(jnp.float32) * (2.0 * math.pi / width)
    factor = 1.0 / math.sqrt(width)
    return (
        (jnp.cos(angle) * factor).astype(jnp.bfloat16),
        (jnp.sin(angle) * factor).astype(jnp.bfloat16),
    )


def polyphase(samples, filter_coeffs, row_gain):
    ntaps = filter_coeffs.shape[0]
    width = filter_coeffs.shape[1]
    grid = samples.astype(jnp.float32).reshape(2, samples.shape[1], -1, width)
    count = grid.shape[2] - ntaps + 1
    filtered = filter_coeffs[0][None, None, None, :] * grid[:, :, 0:count, :]
    for tap_no in range(1, ntaps):
        filtered = (
            filtered
            + filter_coeffs[tap_no][None, None, None, :] * grid[:, :, tap_no : tap_no + count, :]
        )
    return (filtered * row_gain[None, :, None, None]).astype(jnp.bfloat16)


def polyphase_flat(samples, filter_coeffs, row_gain):
    ntaps = filter_coeffs.shape[0]
    width = filter_coeffs.shape[1]
    count = samples.shape[2] // width - ntaps + 1
    span = count * width
    coeffs = jnp.tile(filter_coeffs, (1, count))
    filtered = coeffs[0][None, None, :] * samples[:, :, 0:span].astype(jnp.float32)
    for tap_no in range(1, ntaps):
        window = samples[:, :, tap_no * width : tap_no * width + span].astype(jnp.float32)
        filtered = filtered + coeffs[tap_no][None, None, :] * window
    filtered = (filtered * row_gain[None, :, None]).astype(jnp.bfloat16)
    return filtered.reshape(samples.shape[0], samples.shape[1], count, width)


def transform(filtered, cos_table, sin_table):
    flat_re = filtered[0]
    flat_im = filtered[1]
    dot = lambda a, b: jnp.einsum("stc,ck->stk", a, b, preferred_element_type=jnp.float32)
    out_re = dot(flat_re, cos_table) + dot(flat_im, sin_table)
    out_im = dot(flat_im, cos_table) - dot(flat_re, sin_table)
    return jnp.stack([out_re, out_im]).astype(jnp.bfloat16)


def batched(matrix, vectors):
    return jnp.einsum("ksu,kub->ksb", matrix, vectors, precision=lax.Precision.HIGHEST)


def iterate(rows_re, rows_im, steer_re, steer_im, diag_total, load):
    weight_re = steer_re / diag_total
    weight_im = steer_im / diag_total
    for sweep_no in range(2):
        prod_re = batched(rows_re, weight_re) - batched(rows_im, weight_im)
        prod_im = batched(rows_re, weight_im) + batched(rows_im, weight_re)
        next_re = weight_re + 0.5 * (steer_re - prod_re - load * weight_re) / diag_total
        next_im = weight_im + 0.5 * (steer_im - prod_im - load * weight_im) / diag_total
        weight_re, weight_im = (next_re, next_im)
    return weight_re, weight_im


def local(voltages, filter_coeffs, station_gain, flags, steer_index):
    nblk = lax.axis_size("blk")
    nst = lax.axis_size("st")
    ndev = nblk * nst
    ntaps, nk = filter_coeffs.shape
    cos_table, sin_table = dft_tables(nk)
    row_gain = station_gain * flags[0].astype(jnp.float32)
    samples = voltages[:, 0]
    ls = samples.shape[1]
    nt = samples.shape[2] // nk - ntaps + 1
    kc = nk // ndev
    stations = nst * ls
    counted = nblk * nt
    ngr = 4 if ls % 64 == 0 else 1
    gs = ls // ngr
    me = lax.axis_index("blk") * nst + lax.axis_index("st")
    eye = jnp.eye(stations, dtype=jnp.float32)
    factor = 1.0 / math.sqrt(stations)
    arrived = []
    later = []
    for g in range(ngr):
        part = samples[:, g * gs : (g + 1) * gs]
        filtered = polyphase_flat(part, filter_coeffs, row_gain[g * gs : (g + 1) * gs])
        local_spec = transform(filtered, cos_table, sin_table)
        send = local_spec.reshape(2, gs, nt, ndev, kc).transpose(3, 4, 0, 1, 2)
        if g == 0:
            arrived.append(lax.all_to_all(send, AXES, split_axis=0, concat_axis=0, tiled=True))
        else:
            later.append(send)
    if later:
        later, arrived = lax.optimization_barrier((later, arrived))
    lag = 2
    carries = bool(later) and kc > lag and steer_index.shape[1] // nst == gs

    def channel_send(c, beams_of):
        parts = [part[:, c] for part in later]
        if beams_of is not None:
            parts.append(beams_of)
        return lax.all_to_all(jnp.stack(parts, axis=1), AXES, split_axis=0, concat_axis=0, tiled=True)

    last = {}
    for c in range(min(lag, kc) if carries else kc):
        if later:
            last[c] = channel_send(c, None)
    hi = lax.Precision.HIGHEST
    got = {}
    prev = None
    outs = []
    for c in range(kc):
        pieces = [part[:, c] for part in arrived] + [last[c][:, i] for i in range(len(later))]
        if prev is not None:
            pieces, _ = lax.optimization_barrier((pieces, prev))
        if carries and c >= lag:
            got[c - lag] = last[c][:, len(later)]
        recv = jnp.stack(pieces, axis=2).reshape(nblk, nst, 2, ngr, gs, nt)
        spec = recv.transpose(2, 1, 3, 4, 0, 5).reshape(2 * stations, counted)
        gram = jnp.dot(spec, spec.T, preferred_element_type=jnp.float32)
        g00 = gram[:stations, :stations]
        g01 = gram[:stations, stations:]
        g10 = gram[stations:, :stations]
        g11 = gram[stations:, stations:]
        rows_re = (g00 + g11) / counted
        rows_im = (g10 - g01) / counted
        rows = jnp.concatenate([rows_re, rows_im], axis=0)
        diag_part = jnp.sum(rows_re * eye, axis=1)
        load = jnp.sum(diag_part) / stations + 1e-05
        channel_no = me * kc + c
        phase_int = steer_index * (channel_no + 1) % PHASES
        angle = phase_int.astype(jnp.float32) * (2.0 * math.pi / PHASES)
        steer_re = jnp.cos(angle)
        steer_im = jnp.sin(angle)
        diag_total = (diag_part + load)[:, None]
        weight_re = steer_re / diag_total
        weight_im = steer_im / diag_total
        nb = weight_re.shape[1]
        for sweep_no in range(2):
            both = jnp.concatenate([weight_re, weight_im], axis=1)
            prod = jnp.dot(rows, both, precision=hi)
            prod_re = prod[:stations, :nb] - prod[stations:, nb:]
            prod_im = prod[:stations, nb:] + prod[stations:, :nb]
            next_re = weight_re + 0.5 * (steer_re - prod_re - load * weight_re) / diag_total
            next_im = weight_im + 0.5 * (steer_im - prod_im - load * weight_im) / diag_total
            weight_re, weight_im = (next_re, next_im)
        half_re = weight_re.astype(jnp.bfloat16)
        half_im = weight_im.astype(jnp.bfloat16)
        lhs = jnp.concatenate(
            [jnp.concatenate([half_re, -half_im], axis=1), jnp.concatenate([half_im, half_re], axis=1)],
            axis=0,
        )
        beam = jnp.dot(lhs.T, spec, preferred_element_type=jnp.float32)
        beam = (beam * factor).astype(jnp.bfloat16)
        bc = nb // nst
        out = beam.reshape(2, nst, bc, nblk, nt).transpose(3, 1, 0, 2, 4).reshape(ndev, 2, bc, nt)
        prev = out
        outs.append(out)
        if carries and c + lag < kc:
            last[c + lag] = channel_send(c + lag, out)
    rest = [c for c in range(kc) if c not in got]
    sent = lax.all_to_all(jnp.stack([outs[c] for c in rest], axis=1), AXES, split_axis=0, concat_axis=0, tiled=True)
    for i, c in enumerate(rest):
        got[c] = sent[:, i]
    res = jnp.stack([got[c] for c in range(kc)], axis=4).transpose(1, 2, 3, 0, 4).reshape(2, bc, nt, ndev * kc)
    return res[:, :, None]


def fb_transform(filtered, cos_table, sin_table):
    width = cos_table.shape[0]
    flat_re = filtered[0].reshape(-1, width)
    flat_im = filtered[1].reshape(-1, width)
    out_re = jnp.dot(flat_re, cos_table, preferred_element_type=jnp.float32) + jnp.dot(
        flat_im, sin_table, preferred_element_type=jnp.float32
    )
    out_im = jnp.dot(flat_im, cos_table, preferred_element_type=jnp.float32) - jnp.dot(
        flat_re, sin_table, preferred_element_type=jnp.float32
    )
    return jnp.stack([out_re, out_im]).astype(jnp.bfloat16).reshape(filtered.shape)


def fb_batched(matrix, vectors):
    return jnp.einsum("ksu,kub->ksb", matrix, vectors, precision=lax.Precision.HIGHEST)


def fb_iterate(rows_re, rows_im, steer_re, steer_im, diag_total, load, collect, combine):
    weight_re = steer_re / diag_total
    weight_im = steer_im / diag_total
    for sweep_no in range(2):
        full_re, full_im = collect(weight_re, weight_im)
        prod_re = fb_batched(rows_re, full_re) - fb_batched(rows_im, full_im)
        prod_im = fb_batched(rows_re, full_im) + fb_batched(rows_im, full_re)
        prod_re, prod_im = combine(prod_re, prod_im)
        next_re = weight_re + 0.5 * (steer_re - prod_re - load * weight_re) / diag_total
        next_im = weight_im + 0.5 * (steer_im - prod_im - load * weight_im) / diag_total
        weight_re, weight_im = (next_re, next_im)
    return collect(weight_re, weight_im)


def unchanged(part_re, part_im):
    return (part_re, part_im)


def fb_local(voltages, filter_coeffs, station_gain, flags, steer_index):
    cos_table, sin_table = dft_tables(filter_coeffs.shape[1])
    row_gain = station_gain * flags[0].astype(jnp.float32)
    filtered = polyphase(voltages[:, 0], filter_coeffs, row_gain)
    local_spec = fb_transform(filtered, cos_table, sin_table)
    spectra = lax.all_to_all(local_spec, "st", split_axis=3, concat_axis=1, tiled=True)
    stations = spectra.shape[1]
    chans = spectra.shape[3]
    counted = lax.axis_size("blk") * spectra.shape[2]
    spec_re = spectra[0]
    spec_im = spectra[1]
    cov_re = jnp.einsum(
        "stk,utk->ksu", spec_re, spec_re, preferred_element_type=jnp.float32
    ) + jnp.einsum("stk,utk->ksu", spec_im, spec_im, preferred_element_type=jnp.float32)
    cov_im = jnp.einsum(
        "stk,utk->ksu", spec_im, spec_re, preferred_element_type=jnp.float32
    ) - jnp.einsum("stk,utk->ksu", spec_re, spec_im, preferred_element_type=jnp.float32)
    channel_ids = lax.axis_index("st") * chans + jnp.arange(chans, dtype=jnp.int32)
    total_re, total_im = lax.psum((cov_re, cov_im), "blk")
    rows_re = total_re / counted
    rows_im = total_im / counted
    diag_part = jnp.diagonal(rows_re, axis1=1, axis2=2)
    load = jnp.sum(diag_part, axis=1) / stations + 1e-05
    phase_int = steer_index[None, :, :] * (channel_ids + 1)[:, None, None] % PHASES
    angle = phase_int.astype(jnp.float32) * (2.0 * math.pi / PHASES)
    steer_re = jnp.cos(angle)
    steer_im = jnp.sin(angle)
    load_full = load[:, None, None]
    diag_total = (diag_part + load[:, None])[:, :, None]
    weight_re, weight_im = fb_iterate(
        rows_re, rows_im, steer_re, steer_im, diag_total, load_full, unchanged, unchanged
    )
    half_re = weight_re.astype(jnp.bfloat16)
    half_im = weight_im.astype(jnp.bfloat16)
    beam_re = jnp.einsum(
        "ksb,stk->btk", half_re, spec_re, preferred_element_type=jnp.float32
    ) + jnp.einsum("ksb,stk->btk", half_im, spec_im, preferred_element_type=jnp.float32)
    beam_im = jnp.einsum(
        "ksb,stk->btk", half_re, spec_im, preferred_element_type=jnp.float32
    ) - jnp.einsum("ksb,stk->btk", half_im, spec_re, preferred_element_type=jnp.float32)
    factor = 1.0 / math.sqrt(stations)
    beam_local = (jnp.stack([beam_re, beam_im]) * factor).astype(jnp.bfloat16)
    owned = lax.all_to_all(beam_local, "st", split_axis=1, concat_axis=3, tiled=True)
    return owned[:, :, None]


def body(voltages, filter_coeffs, station_gain, flags, steer_index):
    ndev = lax.axis_size("blk") * lax.axis_size("st")
    plan = local if filter_coeffs.shape[1] % ndev == 0 else fb_local
    return plan(voltages, filter_coeffs, station_gain, flags, steer_index)


def solution(mesh):
    return jax.shard_map(
        body,
        mesh=mesh,
        in_specs=(P(None, "blk", "st", None), P(), P("st"), P("blk", "st"), P()),
        out_specs=P(None, "st", "blk", None, None),
        check_vma=False,
    )
```

```python
import math

import jax
import jax.numpy as jnp
from jax import lax
from jax.sharding import PartitionSpec as P

PHASES = 4096
AXES = ("blk", "st")


def dft_tables(width):
    counter = jnp.arange(width, dtype=jnp.int32)
    product = counter[:, None] * counter[None, :] % width
    angle = product.astype(jnp.float32) * (2.0 * math.pi / width)
    factor = 1.0 / math.sqrt(width)
    return (
        (jnp.cos(angle) * factor).astype(jnp.bfloat16),
        (jnp.sin(angle) * factor).astype(jnp.bfloat16),
    )


def polyphase(samples, filter_coeffs, row_gain):
    ntaps = filter_coeffs.shape[0]
    width = filter_coeffs.shape[1]
    grid = samples.astype(jnp.float32).reshape(2, samples.shape[1], -1, width)
    count = grid.shape[2] - ntaps + 1
    filtered = filter_coeffs[0][None, None, None, :] * grid[:, :, 0:count, :]
    for tap_no in range(1, ntaps):
        filtered = (
            filtered
            + filter_coeffs[tap_no][None, None, None, :] * grid[:, :, tap_no : tap_no + count, :]
        )
    return (filtered * row_gain[None, :, None, None]).astype(jnp.bfloat16)


def polyphase_flat(samples, filter_coeffs, row_gain):
    ntaps = filter_coeffs.shape[0]
    width = filter_coeffs.shape[1]
    count = samples.shape[2] // width - ntaps + 1
    span = count * width
    coeffs = jnp.tile(filter_coeffs, (1, count))
    filtered = coeffs[0][None, None, :] * samples[:, :, 0:span].astype(jnp.float32)
    for tap_no in range(1, ntaps):
        window = samples[:, :, tap_no * width : tap_no * width + span].astype(jnp.float32)
        filtered = filtered + coeffs[tap_no][None, None, :] * window
    filtered = (filtered * row_gain[None, :, None]).astype(jnp.bfloat16)
    return filtered.reshape(samples.shape[0], samples.shape[1], count, width)


def transform(filtered, cos_table, sin_table):
    flat_re = filtered[0]
    flat_im = filtered[1]
    dot = lambda a, b: jnp.einsum("stc,ck->stk", a, b, preferred_element_type=jnp.float32)
    out_re = dot(flat_re, cos_table) + dot(flat_im, sin_table)
    out_im = dot(flat_im, cos_table) - dot(flat_re, sin_table)
    return jnp.stack([out_re, out_im]).astype(jnp.bfloat16)


def batched(matrix, vectors):
    return jnp.einsum("ksu,kub->ksb", matrix, vectors, precision=lax.Precision.HIGHEST)


def iterate(rows_re, rows_im, steer_re, steer_im, diag_total, load):
    weight_re = steer_re / diag_total
    weight_im = steer_im / diag_total
    for sweep_no in range(2):
        prod_re = batched(rows_re, weight_re) - batched(rows_im, weight_im)
        prod_im = batched(rows_re, weight_im) + batched(rows_im, weight_re)
        next_re = weight_re + 0.5 * (steer_re - prod_re - load * weight_re) / diag_total
        next_im = weight_im + 0.5 * (steer_im - prod_im - load * weight_im) / diag_total
        weight_re, weight_im = (next_re, next_im)
    return weight_re, weight_im


def local(voltages, filter_coeffs, station_gain, flags, steer_index):
    nblk = lax.axis_size("blk")
    nst = lax.axis_size("st")
    ndev = nblk * nst
    ntaps, nk = filter_coeffs.shape
    cos_table, sin_table = dft_tables(nk)
    row_gain = station_gain * flags[0].astype(jnp.float32)
    samples = voltages[:, 0]
    ls = samples.shape[1]
    nt = samples.shape[2] // nk - ntaps + 1
    kc = nk // ndev
    stations = nst * ls
    counted = nblk * nt
    ngr = 4 if ls % 64 == 0 else 1
    gs = ls // ngr
    me = lax.axis_index("blk") * nst + lax.axis_index("st")
    eye = jnp.eye(stations, dtype=jnp.float32)
    factor = 1.0 / math.sqrt(stations)
    arrived = []
    later = []
    for g in range(ngr):
        part = samples[:, g * gs : (g + 1) * gs]
        filtered = polyphase_flat(part, filter_coeffs, row_gain[g * gs : (g + 1) * gs])
        local_spec = transform(filtered, cos_table, sin_table)
        send = local_spec.reshape(2, gs, nt, ndev, kc).transpose(3, 4, 0, 1, 2)
        if g == 0:
            arrived.append(lax.all_to_all(send, AXES, split_axis=0, concat_axis=0, tiled=True))
        else:
            later.append(send)
    if later:
        later, arrived = lax.optimization_barrier((later, arrived))
    lag = 2
    carries = bool(later) and kc > lag

    def channel_send(c, after):
        parts = [part[:, c] for part in later]
        if after is not None:
            parts, _ = lax.optimization_barrier((parts, after))
        return lax.all_to_all(jnp.stack(parts, axis=1), AXES, split_axis=0, concat_axis=0, tiled=True)

    last = {}
    for c in range(min(lag, kc) if carries else kc):
        if later:
            last[c] = channel_send(c, None)
    hi = lax.Precision.HIGHEST
    prev = None
    outs = []
    for c in range(kc):
        pieces = [part[:, c] for part in arrived] + [last[c][:, i] for i in range(len(later))]
        if prev is not None:
            pieces, _ = lax.optimization_barrier((pieces, prev))
        recv = jnp.stack(pieces, axis=2).reshape(nblk, nst, 2, ngr, gs, nt)
        spec = recv.transpose(2, 1, 3, 4, 0, 5).reshape(2 * stations, counted)
        gram = jnp.dot(spec, spec.T, preferred_element_type=jnp.float32)
        g00 = gram[:stations, :stations]
        g01 = gram[:stations, stations:]
        g10 = gram[stations:, :stations]
        g11 = gram[stations:, stations:]
        rows_re = (g00 + g11) / counted
        rows_im = (g10 - g01) / counted
        rows = jnp.concatenate([rows_re, rows_im], axis=0)
        diag_part = jnp.sum(rows_re * eye, axis=1)
        load = jnp.sum(diag_part) / stations + 1e-05
        channel_no = me * kc + c
        phase_int = steer_index * (channel_no + 1) % PHASES
        angle = phase_int.astype(jnp.float32) * (2.0 * math.pi / PHASES)
        steer_re = jnp.cos(angle)
        steer_im = jnp.sin(angle)
        diag_total = (diag_part + load)[:, None]
        weight_re = steer_re / diag_total
        weight_im = steer_im / diag_total
        nb = weight_re.shape[1]
        for sweep_no in range(2):
            both = jnp.concatenate([weight_re, weight_im], axis=1)
            prod = jnp.dot(rows, both, precision=hi)
            prod_re = prod[:stations, :nb] - prod[stations:, nb:]
            prod_im = prod[:stations, nb:] + prod[stations:, :nb]
            next_re = weight_re + 0.5 * (steer_re - prod_re - load * weight_re) / diag_total
            next_im = weight_im + 0.5 * (steer_im - prod_im - load * weight_im) / diag_total
            weight_re, weight_im = (next_re, next_im)
        half_re = weight_re.astype(jnp.bfloat16)
        half_im = weight_im.astype(jnp.bfloat16)
        lhs = jnp.concatenate(
            [jnp.concatenate([half_re, -half_im], axis=1), jnp.concatenate([half_im, half_re], axis=1)],
            axis=0,
        )
        beam = jnp.dot(lhs.T, spec, preferred_element_type=jnp.float32)
        beam = (beam * factor).astype(jnp.bfloat16)
        bc = nb // nst
        out = beam.reshape(2, nst, bc, nblk, nt).transpose(3, 1, 0, 2, 4).reshape(ndev, 2, bc, nt)
        prev = out
        outs.append(out)
        if carries and c + lag < kc:
            last[c + lag] = channel_send(c + lag, out)
    sent = lax.all_to_all(jnp.stack(outs, axis=1), AXES, split_axis=0, concat_axis=0, tiled=True)
    res = sent.transpose(2, 3, 4, 0, 1).reshape(2, bc, nt, ndev * kc)
    return res[:, :, None]


def fb_transform(filtered, cos_table, sin_table):
    width = cos_table.shape[0]
    flat_re = filtered[0].reshape(-1, width)
    flat_im = filtered[1].reshape(-1, width)
    out_re = jnp.dot(flat_re, cos_table, preferred_element_type=jnp.float32) + jnp.dot(
        flat_im, sin_table, preferred_element_type=jnp.float32
    )
    out_im = jnp.dot(flat_im, cos_table, preferred_element_type=jnp.float32) - jnp.dot(
        flat_re, sin_table, preferred_element_type=jnp.float32
    )
    return jnp.stack([out_re, out_im]).astype(jnp.bfloat16).reshape(filtered.shape)


def fb_batched(matrix, vectors):
    return jnp.einsum("ksu,kub->ksb", matrix, vectors, precision=lax.Precision.HIGHEST)


def fb_iterate(rows_re, rows_im, steer_re, steer_im, diag_total, load, collect, combine):
    weight_re = steer_re / diag_total
    weight_im = steer_im / diag_total
    for sweep_no in range(2):
        full_re, full_im = collect(weight_re, weight_im)
        prod_re = fb_batched(rows_re, full_re) - fb_batched(rows_im, full_im)
        prod_im = fb_batched(rows_re, full_im) + fb_batched(rows_im, full_re)
        prod_re, prod_im = combine(prod_re, prod_im)
        next_re = weight_re + 0.5 * (steer_re - prod_re - load * weight_re) / diag_total
        next_im = weight_im + 0.5 * (steer_im - prod_im - load * weight_im) / diag_total
        weight_re, weight_im = (next_re, next_im)
    return collect(weight_re, weight_im)


def unchanged(part_re, part_im):
    return (part_re, part_im)


def fb_local(voltages, filter_coeffs, station_gain, flags, steer_index):
    cos_table, sin_table = dft_tables(filter_coeffs.shape[1])
    row_gain = station_gain * flags[0].astype(jnp.float32)
    filtered = polyphase(voltages[:, 0], filter_coeffs, row_gain)
    local_spec = fb_transform(filtered, cos_table, sin_table)
    spectra = lax.all_to_all(local_spec, "st", split_axis=3, concat_axis=1, tiled=True)
    stations = spectra.shape[1]
    chans = spectra.shape[3]
    counted = lax.axis_size("blk") * spectra.shape[2]
    spec_re = spectra[0]
    spec_im = spectra[1]
    cov_re = jnp.einsum(
        "stk,utk->ksu", spec_re, spec_re, preferred_element_type=jnp.float32
    ) + jnp.einsum("stk,utk->ksu", spec_im, spec_im, preferred_element_type=jnp.float32)
    cov_im = jnp.einsum(
        "stk,utk->ksu", spec_im, spec_re, preferred_element_type=jnp.float32
    ) - jnp.einsum("stk,utk->ksu", spec_re, spec_im, preferred_element_type=jnp.float32)
    channel_ids = lax.axis_index("st") * chans + jnp.arange(chans, dtype=jnp.int32)
    total_re, total_im = lax.psum((cov_re, cov_im), "blk")
    rows_re = total_re / counted
    rows_im = total_im / counted
    diag_part = jnp.diagonal(rows_re, axis1=1, axis2=2)
    load = jnp.sum(diag_part, axis=1) / stations + 1e-05
    phase_int = steer_index[None, :, :] * (channel_ids + 1)[:, None, None] % PHASES
    angle = phase_int.astype(jnp.float32) * (2.0 * math.pi / PHASES)
    steer_re = jnp.cos(angle)
    steer_im = jnp.sin(angle)
    load_full = load[:, None, None]
    diag_total = (diag_part + load[:, None])[:, :, None]
    weight_re, weight_im = fb_iterate(
        rows_re, rows_im, steer_re, steer_im, diag_total, load_full, unchanged, unchanged
    )
    half_re = weight_re.astype(jnp.bfloat16)
    half_im = weight_im.astype(jnp.bfloat16)
    beam_re = jnp.einsum(
        "ksb,stk->btk", half_re, spec_re, preferred_element_type=jnp.float32
    ) + jnp.einsum("ksb,stk->btk", half_im, spec_im, preferred_element_type=jnp.float32)
    beam_im = jnp.einsum(
        "ksb,stk->btk", half_re, spec_im, preferred_element_type=jnp.float32
    ) - jnp.einsum("ksb,stk->btk", half_im, spec_re, preferred_element_type=jnp.float32)
    factor = 1.0 / math.sqrt(stations)
    beam_local = (jnp.stack([beam_re, beam_im]) * factor).astype(jnp.bfloat16)
    owned = lax.all_to_all(beam_local, "st", split_axis=1, concat_axis=3, tiled=True)
    return owned[:, :, None]


def body(voltages, filter_coeffs, station_gain, flags, steer_index):
    ndev = lax.axis_size("blk") * lax.axis_size("st")
    plan = local if filter_coeffs.shape[1] % ndev == 0 else fb_local
    return plan(voltages, filter_coeffs, station_gain, flags, steer_index)


def solution(mesh):
    return jax.shard_map(
        body,
        mesh=mesh,
        in_specs=(P(None, "blk", "st", None), P(), P("st"), P("blk", "st"), P()),
        out_specs=P(None, "st", "blk", None, None),
        check_vma=False,
    )
```

```python
import math

import jax
import jax.numpy as jnp
from jax import lax
from jax.sharding import PartitionSpec as P

PHASES = 4096
AXES = ("blk", "st")


def dft_tables(width):
    counter = jnp.arange(width, dtype=jnp.int32)
    product = counter[:, None] * counter[None, :] % width
    angle = product.astype(jnp.float32) * (2.0 * math.pi / width)
    factor = 1.0 / math.sqrt(width)
    return (
        (jnp.cos(angle) * factor).astype(jnp.bfloat16),
        (jnp.sin(angle) * factor).astype(jnp.bfloat16),
    )


def polyphase(samples, filter_coeffs, row_gain):
    ntaps = filter_coeffs.shape[0]
    width = filter_coeffs.shape[1]
    grid = samples.astype(jnp.float32).reshape(2, samples.shape[1], -1, width)
    count = grid.shape[2] - ntaps + 1
    filtered = filter_coeffs[0][None, None, None, :] * grid[:, :, 0:count, :]
    for tap_no in range(1, ntaps):
        filtered = (
            filtered
            + filter_coeffs[tap_no][None, None, None, :] * grid[:, :, tap_no : tap_no + count, :]
        )
    return (filtered * row_gain[None, :, None, None]).astype(jnp.bfloat16)


def polyphase_flat(samples, filter_coeffs, row_gain):
    ntaps = filter_coeffs.shape[0]
    width = filter_coeffs.shape[1]
    count = samples.shape[2] // width - ntaps + 1
    span = count * width
    coeffs = jnp.tile(filter_coeffs, (1, count))
    filtered = coeffs[0][None, None, :] * samples[:, :, 0:span].astype(jnp.float32)
    for tap_no in range(1, ntaps):
        window = samples[:, :, tap_no * width : tap_no * width + span].astype(jnp.float32)
        filtered = filtered + coeffs[tap_no][None, None, :] * window
    filtered = (filtered * row_gain[None, :, None]).astype(jnp.bfloat16)
    return filtered.reshape(samples.shape[0], samples.shape[1], count, width)


def transform(filtered, cos_table, sin_table):
    flat_re = filtered[0]
    flat_im = filtered[1]
    dot = lambda a, b: jnp.einsum("stc,ck->stk", a, b, preferred_element_type=jnp.float32)
    out_re = dot(flat_re, cos_table) + dot(flat_im, sin_table)
    out_im = dot(flat_im, cos_table) - dot(flat_re, sin_table)
    return jnp.stack([out_re, out_im]).astype(jnp.bfloat16)


def batched(matrix, vectors):
    return jnp.einsum("ksu,kub->ksb", matrix, vectors, precision=lax.Precision.HIGHEST)


def iterate(rows_re, rows_im, steer_re, steer_im, diag_total, load):
    weight_re = steer_re / diag_total
    weight_im = steer_im / diag_total
    for sweep_no in range(2):
        prod_re = batched(rows_re, weight_re) - batched(rows_im, weight_im)
        prod_im = batched(rows_re, weight_im) + batched(rows_im, weight_re)
        next_re = weight_re + 0.5 * (steer_re - prod_re - load * weight_re) / diag_total
        next_im = weight_im + 0.5 * (steer_im - prod_im - load * weight_im) / diag_total
        weight_re, weight_im = (next_re, next_im)
    return weight_re, weight_im


def local(voltages, filter_coeffs, station_gain, flags, steer_index):
    nblk = lax.axis_size("blk")
    nst = lax.axis_size("st")
    ndev = nblk * nst
    ntaps, nk = filter_coeffs.shape
    cos_table, sin_table = dft_tables(nk)
    row_gain = station_gain * flags[0].astype(jnp.float32)
    samples = voltages[:, 0]
    ls = samples.shape[1]
    nt = samples.shape[2] // nk - ntaps + 1
    kc = nk // ndev
    stations = nst * ls
    counted = nblk * nt
    ngr = 4 if ls % 64 == 0 else 1
    gs = ls // ngr
    me = lax.axis_index("blk") * nst + lax.axis_index("st")
    eye = jnp.eye(stations, dtype=jnp.float32)
    factor = 1.0 / math.sqrt(stations)
    arrived = []
    later = []
    for g in range(ngr):
        part = samples[:, g * gs : (g + 1) * gs]
        filtered = polyphase_flat(part, filter_coeffs, row_gain[g * gs : (g + 1) * gs])
        local_spec = transform(filtered, cos_table, sin_table)
        send = local_spec.reshape(2, gs, nt, ndev, kc).transpose(3, 4, 0, 1, 2)
        if g == 0:
            arrived.append(lax.all_to_all(send, AXES, split_axis=0, concat_axis=0, tiled=True))
        else:
            later.append(send)
    if later:
        later, arrived = lax.optimization_barrier((later, arrived))
    last = [
        lax.all_to_all(
            jnp.stack([part[:, c] for part in later], axis=1), AXES, split_axis=0, concat_axis=0, tiled=True
        )
        for c in range(kc)
        if later
    ]
    hi = lax.Precision.HIGHEST
    channel_nos = me * kc + jnp.arange(kc, dtype=jnp.int32)
    phase_all = steer_index[None, :, :] * (channel_nos + 1)[:, None, None] % PHASES
    angle_all = phase_all.astype(jnp.float32) * (2.0 * math.pi / PHASES)
    steer_all_re = jnp.cos(angle_all)
    steer_all_im = jnp.sin(angle_all)
    got = []
    prev = None
    for c in range(kc):
        pieces = [part[:, c] for part in arrived] + [last[c][:, i] for i in range(len(later))]
        if prev is not None:
            pieces, _ = lax.optimization_barrier((pieces, prev))
        recv = jnp.stack(pieces, axis=2).reshape(nblk, nst, 2, ngr, gs, nt)
        spec = recv.transpose(2, 1, 3, 4, 0, 5).reshape(2 * stations, counted)
        gram = jnp.dot(spec, spec.T, preferred_element_type=jnp.float32)
        g00 = gram[:stations, :stations]
        g01 = gram[:stations, stations:]
        g10 = gram[stations:, :stations]
        g11 = gram[stations:, stations:]
        rows_re = (g00 + g11) / counted
        rows_im = (g10 - g01) / counted
        rows = jnp.concatenate([rows_re, rows_im], axis=0)
        diag_part = jnp.sum(rows_re * eye, axis=1)
        load = jnp.sum(diag_part) / stations + 1e-05
        steer_re = steer_all_re[c]
        steer_im = steer_all_im[c]
        diag_total = (diag_part + load)[:, None]
        weight_re = steer_re / diag_total
        weight_im = steer_im / diag_total
        nb = weight_re.shape[1]
        for sweep_no in range(2):
            both = jnp.concatenate([weight_re, weight_im], axis=1)
            prod = jnp.dot(rows, both, precision=hi)
            prod_re = prod[:stations, :nb] - prod[stations:, nb:]
            prod_im = prod[:stations, nb:] + prod[stations:, :nb]
            next_re = weight_re + 0.5 * (steer_re - prod_re - load * weight_re) / diag_total
            next_im = weight_im + 0.5 * (steer_im - prod_im - load * weight_im) / diag_total
            weight_re, weight_im = (next_re, next_im)
        half_re = weight_re.astype(jnp.bfloat16)
        half_im = weight_im.astype(jnp.bfloat16)
        lhs = jnp.concatenate(
            [jnp.concatenate([half_re, -half_im], axis=1), jnp.concatenate([half_im, half_re], axis=1)],
            axis=0,
        )
        beam = jnp.dot(lhs.T, spec, preferred_element_type=jnp.float32)
        beam = (beam * factor).astype(jnp.bfloat16)
        bc = nb // nst
        out = beam.reshape(2, nst, bc, nblk, nt).transpose(3, 1, 0, 2, 4).reshape(ndev, 2, bc, nt)
        prev = out
        got.append(lax.all_to_all(out, AXES, split_axis=0, concat_axis=0, tiled=True))
    res = jnp.stack(got, axis=4).transpose(1, 2, 3, 0, 4).reshape(2, bc, nt, ndev * kc)
    return res[:, :, None]


def fb_transform(filtered, cos_table, sin_table):
    width = cos_table.shape[0]
    flat_re = filtered[0].reshape(-1, width)
    flat_im = filtered[1].reshape(-1, width)
    out_re = jnp.dot(flat_re, cos_table, preferred_element_type=jnp.float32) + jnp.dot(
        flat_im, sin_table, preferred_element_type=jnp.float32
    )
    out_im = jnp.dot(flat_im, cos_table, preferred_element_type=jnp.float32) - jnp.dot(
        flat_re, sin_table, preferred_element_type=jnp.float32
    )
    return jnp.stack([out_re, out_im]).astype(jnp.bfloat16).reshape(filtered.shape)


def fb_batched(matrix, vectors):
    return jnp.einsum("ksu,kub->ksb", matrix, vectors, precision=lax.Precision.HIGHEST)


def fb_iterate(rows_re, rows_im, steer_re, steer_im, diag_total, load, collect, combine):
    weight_re = steer_re / diag_total
    weight_im = steer_im / diag_total
    for sweep_no in range(2):
        full_re, full_im = collect(weight_re, weight_im)
        prod_re = fb_batched(rows_re, full_re) - fb_batched(rows_im, full_im)
        prod_im = fb_batched(rows_re, full_im) + fb_batched(rows_im, full_re)
        prod_re, prod_im = combine(prod_re, prod_im)
        next_re = weight_re + 0.5 * (steer_re - prod_re - load * weight_re) / diag_total
        next_im = weight_im + 0.5 * (steer_im - prod_im - load * weight_im) / diag_total
        weight_re, weight_im = (next_re, next_im)
    return collect(weight_re, weight_im)


def unchanged(part_re, part_im):
    return (part_re, part_im)


def fb_local(voltages, filter_coeffs, station_gain, flags, steer_index):
    cos_table, sin_table = dft_tables(filter_coeffs.shape[1])
    row_gain = station_gain * flags[0].astype(jnp.float32)
    filtered = polyphase(voltages[:, 0], filter_coeffs, row_gain)
    local_spec = fb_transform(filtered, cos_table, sin_table)
    spectra = lax.all_to_all(local_spec, "st", split_axis=3, concat_axis=1, tiled=True)
    stations = spectra.shape[1]
    chans = spectra.shape[3]
    counted = lax.axis_size("blk") * spectra.shape[2]
    spec_re = spectra[0]
    spec_im = spectra[1]
    cov_re = jnp.einsum(
        "stk,utk->ksu", spec_re, spec_re, preferred_element_type=jnp.float32
    ) + jnp.einsum("stk,utk->ksu", spec_im, spec_im, preferred_element_type=jnp.float32)
    cov_im = jnp.einsum(
        "stk,utk->ksu", spec_im, spec_re, preferred_element_type=jnp.float32
    ) - jnp.einsum("stk,utk->ksu", spec_re, spec_im, preferred_element_type=jnp.float32)
    channel_ids = lax.axis_index("st") * chans + jnp.arange(chans, dtype=jnp.int32)
    total_re, total_im = lax.psum((cov_re, cov_im), "blk")
    rows_re = total_re / counted
    rows_im = total_im / counted
    diag_part = jnp.diagonal(rows_re, axis1=1, axis2=2)
    load = jnp.sum(diag_part, axis=1) / stations + 1e-05
    phase_int = steer_index[None, :, :] * (channel_ids + 1)[:, None, None] % PHASES
    angle = phase_int.astype(jnp.float32) * (2.0 * math.pi / PHASES)
    steer_re = jnp.cos(angle)
    steer_im = jnp.sin(angle)
    load_full = load[:, None, None]
    diag_total = (diag_part + load[:, None])[:, :, None]
    weight_re, weight_im = fb_iterate(
        rows_re, rows_im, steer_re, steer_im, diag_total, load_full, unchanged, unchanged
    )
    half_re = weight_re.astype(jnp.bfloat16)
    half_im = weight_im.astype(jnp.bfloat16)
    beam_re = jnp.einsum(
        "ksb,stk->btk", half_re, spec_re, preferred_element_type=jnp.float32
    ) + jnp.einsum("ksb,stk->btk", half_im, spec_im, preferred_element_type=jnp.float32)
    beam_im = jnp.einsum(
        "ksb,stk->btk", half_re, spec_im, preferred_element_type=jnp.float32
    ) - jnp.einsum("ksb,stk->btk", half_im, spec_re, preferred_element_type=jnp.float32)
    factor = 1.0 / math.sqrt(stations)
    beam_local = (jnp.stack([beam_re, beam_im]) * factor).astype(jnp.bfloat16)
    owned = lax.all_to_all(beam_local, "st", split_axis=1, concat_axis=3, tiled=True)
    return owned[:, :, None]


def body(voltages, filter_coeffs, station_gain, flags, steer_index):
    ndev = lax.axis_size("blk") * lax.axis_size("st")
    plan = local if filter_coeffs.shape[1] % ndev == 0 else fb_local
    return plan(voltages, filter_coeffs, station_gain, flags, steer_index)


def solution(mesh):
    return jax.shard_map(
        body,
        mesh=mesh,
        in_specs=(P(None, "blk", "st", None), P(), P("st"), P("blk", "st"), P()),
        out_specs=P(None, "st", "blk", None, None),
        check_vma=False,
    )
```
